1024 devices in a mesh: phase: 2 (over core), px: 8 (over y), py: 64 (over z, x).
Axes of the slice: x: 8, y: 8, z: 8, core: 2. Of those that a mesh axis runs over, the one named last changes fastest.
Arguments:
- node_latents: bfloat16 [2, 8, 64, 128, 256], P(None, 'px', 'py'), may hold values from -6 to 6
- edge_latents: bfloat16 [2, 8, 64, 5, 64, 256], P(None, 'px', 'py'), may hold values from -6 to 6
- tile_offsets: int32 [8, 64, 5], P('px', 'py'), may hold values from 0 to 8, as said below
- edge_dst: int32 [8, 64, 5, 64], P('px', 'py'), may hold values from 0 to 127
- edge_src: int32 [8, 64, 5, 64], P('px', 'py'), may hold values from 0 to 127
- edge_in_w: bfloat16 [2, 768, 256], P('phase'), may hold values from -0.21875 to 0.21875
- edge_out_w: bfloat16 [2, 256, 256], P('phase'), may hold values from -0.375 to 0.375
- node_in_w: bfloat16 [2, 512, 256], P('phase'), may hold values from -0.25 to 0.25
- node_out_w: bfloat16 [2, 256, 256], P('phase'), may hold values from -0.375 to 0.375
- node_cot: bfloat16 [2, 8, 64, 128, 256], P(None, 'px', 'py'), may hold values from -6 to 6
- edge_cot: bfloat16 [2, 8, 64, 5, 64, 256], P(None, 'px', 'py'), may hold values from -6 to 6
Outputs:
- node_out: bfloat16 [2, 2, 8, 64, 128, 256], P('phase', None, 'px', 'py')
- edge_out: bfloat16 [2, 2, 8, 64, 5, 64, 256], P('phase', None, 'px', 'py')
- node_grad: float32 [2, 2, 8, 64, 128, 256], P('phase', None, 'px', 'py')
- edge_grad: float32 [2, 2, 8, 64, 5, 64, 256], P('phase', None, 'px', 'py')
The draws below stay inside these ranges and needn't reach their ends.
Inputs may be any that keep to these rules, and one draw needn't show every extreme that they name: `tile_offsets`: code c names the source block (a + c // 3 - 1, b + c % 3 - 1). Tile 0 of every destination block may take any code; tiles 1, 2, 3, 4 take codes from the finite set (0, 1, 2), the finite set (6, 7, 8), the finite set (0, 3, 6) and the finite set (2, 5, 8) respectively.
All inputs are finite; a program needn't handle non-finite values.
Results may differ from the reference program's by a relative error of at most 0.014.
Values may be sent and summed in bfloat16 or wider, within the bound.
No kernel may reach another device: no remote copies, remote signals or barrier semaphores. Data moves between devices by JAX's collectives and lax.ppermute only.
A program may use at most 32 MiB of HBM per device.

```python
import jax
import jax.numpy as jnp
from jax import lax

D = 256
BLK = 128
TPB = 5
EPT = 64
MB = 2
GX = 8
GY = 64


def draw_tile_offsets(key, part):
    subkeys = jax.random.split(key, 3)
    free_code = jax.random.randint(subkeys[0], (GX, GY, 1), 0, 9)
    sideways = jax.random.randint(subkeys[1], (GX, GY, 2), 0, 3)
    vertical = jax.random.randint(subkeys[2], (GX, GY, 2), 0, 3)
    upward_code = sideways[..., 0:1]
    downward_code = 6 + sideways[..., 1:2]
    leftward_code = 3 * vertical[..., 0:1]
    rightward_code = 3 * vertical[..., 1:2] + 2
    return jnp.concatenate([free_code, upward_code, downward_code, leftward_code, rightward_code], axis=-1).astype(jnp.int32)


def plant(entries, own_key, least, top_value):
    spot = [jax.random.randint(jax.random.fold_in(own_key, axis), (), 0, length) for axis, length in enumerate(entries.shape)]
    longest = entries.shape.index(max(entries.shape))
    neighbour = spot[:longest] + [(spot[longest] + 1) % entries.shape[longest]] + spot[longest + 1:]
    return entries.at[tuple(spot)].set(least).at[tuple(neighbour)].set(top_value)


def steps_of(rng, extent, cuts, smallest, high):
    def one(position, blocks):
        heights = jax.random.uniform(jax.random.fold_in(jax.random.fold_in(rng, 6), position), (blocks,), jnp.float32, smallest / len(cuts), high / len(cuts))
        return jnp.repeat(jnp.exp(heights), extent[position] // blocks).reshape((-1,) + (1,) * (len(extent) - position - 1))

    loudness = one(*cuts[0])
    for cut in cuts[1:]:
        loudness = loudness * one(*cut)
    return loudness


def bell_draw(own_key, shape, spread, reach, cuts=(), dtype=jnp.bfloat16):
    entries = jax.random.normal(own_key, shape, jnp.float32) * spread
    if len(cuts) > 0:
        entries = steps_of(own_key, shape, cuts, -0.22, 0.18) * entries
    return jnp.clip(entries, min=-reach, max=reach).astype(dtype)


def setup_inputs(seed: int = 0) -> dict:
    arg_keys = jax.random.split(jax.random.key(seed), 12)
    return {
        "node_latents": bell_draw(arg_keys[0], (MB, GX, GY, BLK, D), 1.0, 6.0, ((1, 8), (2, 64))),
        "edge_latents": bell_draw(arg_keys[1], (MB, GX, GY, TPB, EPT, D), 1.0, 6.0, ((1, 8), (2, 64))),
        "tile_offsets": draw_tile_offsets(jax.random.fold_in(arg_keys[11], 71), 0),
        "edge_dst": plant(jax.random.randint(arg_keys[3], (GX, GY, TPB, EPT), 0, BLK), jax.random.fold_in(arg_keys[3], 1), 0, BLK - 1).astype(jnp.int32),
        "edge_src": plant(jax.random.randint(arg_keys[4], (GX, GY, TPB, EPT), 0, BLK), jax.random.fold_in(arg_keys[4], 1), 0, BLK - 1).astype(jnp.int32),
        "edge_in_w": bell_draw(arg_keys[5], (2, 3 * D, D), (3 * D) ** -0.5, 0.21875, ((0, 2),)),
        "edge_out_w": bell_draw(arg_keys[6], (2, D, D), D ** -0.5, 0.375, ((0, 2),)),
        "node_in_w": bell_draw(arg_keys[7], (2, 2 * D, D), (2 * D) ** -0.5, 0.25, ((0, 2),)),
        "node_out_w": bell_draw(arg_keys[8], (2, D, D), D ** -0.5, 0.375, ((0, 2),)),
        "node_cot": bell_draw(arg_keys[9], (MB, GX, GY, BLK, D), 1.0, 6.0, ((1, 8), (2, 64))),
        "edge_cot": bell_draw(arg_keys[10], (MB, GX, GY, TPB, EPT, D), 1.0, 6.0, ((1, 8), (2, 64))),
    }


def normalize(values):
    centred = values - lax.optimization_barrier(jnp.mean(values, axis=-1, keepdims=True))
    inverse = lax.rsqrt(lax.optimization_barrier(jnp.mean(centred * centred, axis=-1, keepdims=True)) + 1e-05)
    return (centred * inverse, inverse)

def norm_back(values, upstream):
    normed, inverse = normalize(values)
    return inverse * (upstream - lax.optimization_barrier(jnp.mean(upstream, axis=-1, keepdims=True)) - normed * lax.optimization_barrier(jnp.mean(upstream * normed, axis=-1, keepdims=True)))

def silu_slope(values):
    squash = jax.nn.sigmoid(values)
    return squash * (1.0 + values * (1.0 - squash))

def forward(weights, node_flat, edge_flat, source_table, dst_index, src_index):
    edge_in, edge_outer, node_in, node_outer = weights
    joined = jnp.concatenate([edge_flat, node_flat[dst_index], source_table[src_index]], axis=1)
    act_edge = jnp.dot(joined, edge_in, preferred_element_type=jnp.float32)
    hidden_edge = jax.nn.silu(act_edge).astype(jnp.bfloat16)
    edge_pre = jnp.dot(hidden_edge, edge_outer, preferred_element_type=jnp.float32)
    message = normalize(edge_pre)[0]
    edge_new = (edge_flat.astype(jnp.float32) + message).astype(jnp.bfloat16)
    summed = jax.ops.segment_sum(message, dst_index, num_segments=node_flat.shape[0]).astype(jnp.bfloat16)
    node_joined = jnp.concatenate([node_flat, summed], axis=1)
    act_node = jnp.dot(node_joined, node_in, preferred_element_type=jnp.float32)
    hidden_node = jax.nn.silu(act_node).astype(jnp.bfloat16)
    node_pre = jnp.dot(hidden_node, node_outer, preferred_element_type=jnp.float32)
    node_new = (node_flat.astype(jnp.float32) + normalize(node_pre)[0]).astype(jnp.bfloat16)
    return (node_new, edge_new, (act_edge, edge_pre, act_node, node_pre))

def backward(weights, kept_values, grad_node, grad_edge, dst_index, src_index, table_rows):
    edge_in, edge_outer, node_in, node_outer = weights
    act_edge, edge_pre, act_node, node_pre = kept_values
    feature_width = grad_node.shape[1]
    pre_node_grad = norm_back(node_pre, grad_node).astype(jnp.bfloat16)
    hidden_node_grad = jnp.dot(pre_node_grad, node_outer.T, preferred_element_type=jnp.float32)
    act_node_grad = (hidden_node_grad * silu_slope(act_node)).astype(jnp.bfloat16)
    joined_node_grad = jnp.dot(act_node_grad, node_in.T, preferred_element_type=jnp.float32)
    message_grad = grad_edge + joined_node_grad[:, feature_width:][dst_index]
    pre_edge_grad = norm_back(edge_pre, message_grad).astype(jnp.bfloat16)
    hidden_edge_grad = jnp.dot(pre_edge_grad, edge_outer.T, preferred_element_type=jnp.float32)
    act_edge_grad = (hidden_edge_grad * silu_slope(act_edge)).astype(jnp.bfloat16)
    joined_edge_grad = jnp.dot(act_edge_grad, edge_in.T, preferred_element_type=jnp.float32)
    edge_back = grad_edge + joined_edge_grad[:, :feature_width]
    node_back = grad_node + joined_node_grad[:, :feature_width] + jax.ops.segment_sum(joined_edge_grad[:, feature_width:2 * feature_width], dst_index, num_segments=grad_node.shape[0])
    table_back = jax.ops.segment_sum(joined_edge_grad[:, 2 * feature_width:], src_index, num_segments=table_rows)
    return (node_back, edge_back, table_back)

def one_window(node_latents, edge_latents, tile_offsets, edge_dst, edge_src, edge_in_w, edge_out_w, node_in_w, node_out_w, node_cot, edge_cot):
    rows_x = node_latents.shape[0]
    rows_y = node_latents.shape[1]
    block_nodes = node_latents.shape[2]
    feature_width = node_latents.shape[3]
    step_x = tile_offsets // 3 - 1
    step_y = tile_offsets % 3 - 1
    block_x = lax.broadcasted_iota(jnp.int32, tile_offsets.shape, 0)
    block_y = lax.broadcasted_iota(jnp.int32, tile_offsets.shape, 1)
    source_block = (block_x + 1 + step_x) * (rows_y + 2) + block_y + 1 + step_y
    src_index = (source_block[..., None] * block_nodes + edge_src).reshape(-1).astype(jnp.int32)
    dst_index = ((block_x * rows_y + block_y)[..., None] * block_nodes + edge_dst).reshape(-1).astype(jnp.int32)
    table_rows = (rows_x + 2) * (rows_y + 2) * block_nodes

    def padded(node_flat):
        node_grid = node_flat.reshape(rows_x, rows_y, block_nodes, feature_width)
        return jnp.pad(node_grid, ((1, 1), (1, 1), (0, 0), (0, 0))).reshape(-1, feature_width)

    def cropped(table_back):
        table_grid = table_back.reshape(rows_x + 2, rows_y + 2, block_nodes, feature_width)
        return table_grid[1:-1, 1:-1].reshape(-1, feature_width)

    def layer_weights(section):
        return (edge_in_w[section], edge_out_w[section], node_in_w[section], node_out_w[section])
    node_zero = node_latents.reshape(-1, feature_width)
    edge_zero = edge_latents.reshape(-1, feature_width)
    node_one, edge_one, kept_one = forward(layer_weights(0), node_zero, edge_zero, padded(node_zero), dst_index, src_index)
    node_two, edge_two, kept_two = forward(layer_weights(1), node_one, edge_one, padded(node_one), dst_index, src_index)
    node_back_one, edge_back_one, table_one = backward(layer_weights(1), kept_two, node_cot.reshape(-1, feature_width).astype(jnp.float32), edge_cot.reshape(-1, feature_width).astype(jnp.float32), dst_index, src_index, table_rows)
    node_back_one = node_back_one + cropped(table_one)
    node_back_zero, edge_back_zero, table_zero = backward(layer_weights(0), kept_one, node_back_one, edge_back_one, dst_index, src_index, table_rows)
    node_back_zero = node_back_zero + cropped(table_zero)
    node_shape = (2,) + node_latents.shape
    edge_shape = (2,) + edge_latents.shape
    return (jnp.stack([node_one, node_two]).reshape(node_shape), jnp.stack([edge_one, edge_two]).reshape(edge_shape), jnp.stack([node_back_zero, node_back_one]).reshape(node_shape), jnp.stack([edge_back_zero, edge_back_one]).reshape(edge_shape))

def reference(node_latents, edge_latents, tile_offsets, edge_dst, edge_src, edge_in_w, edge_out_w, node_in_w, node_out_w, node_cot, edge_cot):
    results = []
    for window in range(node_latents.shape[0]):
        results.append(one_window(node_latents[window], edge_latents[window], tile_offsets, edge_dst, edge_src, edge_in_w, edge_out_w, node_in_w, node_out_w, node_cot[window], edge_cot[window]))
    return (jnp.stack([item[0] for item in results], axis=1), jnp.stack([item[1] for item in results], axis=1), jnp.stack([item[2] for item in results], axis=1), jnp.stack([item[3] for item in results], axis=1))
```

```python
import jax
import jax.numpy as jnp
from jax import lax
from jax.sharding import PartitionSpec as P


def shifted(array, axis, by):
    count = lax.axis_size(axis)
    pairs = [(i, i + by) for i in range(count) if 0 <= i + by < count]
    return lax.ppermute(array, axis, pairs)


def normalize(values):
    centred = values - jnp.mean(values, axis=-1, keepdims=True)
    inverse = lax.rsqrt(jnp.mean(centred * centred, axis=-1, keepdims=True) + 1e-05)
    return (centred * inverse, inverse)


def norm_back(values, upstream):
    normed, inverse = normalize(values)
    return inverse * (
        upstream
        - jnp.mean(upstream, axis=-1, keepdims=True)
        - normed * jnp.mean(upstream * normed, axis=-1, keepdims=True)
    )


def silu_slope(values):
    squash = jax.nn.sigmoid(values)
    return squash * (1.0 + values * (1.0 - squash))


def times_plain(left, right):
    return jnp.einsum("mrk,kd->mrd", left, right, preferred_element_type=jnp.float32)


def times_turned(left, right):
    return jnp.einsum("mrd,kd->mrk", left, right, preferred_element_type=jnp.float32)


def exact_sum(form, left, right):
    return jnp.einsum(
        form, left, right, precision=lax.Precision.HIGHEST, preferred_element_type=jnp.float32
    )


def neighbourhood(node_blocks):
    column = jnp.stack(
        [shifted(node_blocks, "px", 1), node_blocks, shifted(node_blocks, "px", -1)], axis=1
    )
    grid = jnp.stack([shifted(column, "py", 1), column, shifted(column, "py", -1)], axis=2)
    return grid.reshape((grid.shape[0], 9) + grid.shape[3:])


def return_to_owners(table_back):
    grid = table_back.reshape((table_back.shape[0], 3, 3) + table_back.shape[2:])
    low = grid[:, :, 0].astype(jnp.bfloat16)
    high = grid[:, :, 2].astype(jnp.bfloat16)
    column = (
        grid[:, :, 1]
        + shifted(low, "py", -1).astype(jnp.float32)
        + shifted(high, "py", 1).astype(jnp.float32)
    )
    low = column[:, 0].astype(jnp.bfloat16)
    high = column[:, 2].astype(jnp.bfloat16)
    return (
        column[:, 1]
        + shifted(low, "px", -1).astype(jnp.float32)
        + shifted(high, "px", 1).astype(jnp.float32)
    )


def forward(weights, tables, node_blocks, edge_rows):
    edge_in, edge_outer, node_in, node_outer = weights
    dst_onehot, src_onehot, block_pick = tables
    windows, block_nodes, width = node_blocks.shape
    tiles, edges_tile = dst_onehot.shape[:2]
    source_table = neighbourhood(node_blocks)
    at_dst = jnp.einsum(
        "tkn,mnd->mtkd", dst_onehot, node_blocks, preferred_element_type=jnp.float32
    ).astype(jnp.bfloat16)
    src_blocks = jnp.einsum(
        "tb,mbnd->mtnd", block_pick.astype(jnp.bfloat16), source_table,
        preferred_element_type=jnp.float32,
    ).astype(jnp.bfloat16)
    at_src = jnp.einsum(
        "tkn,mtnd->mtkd", src_onehot, src_blocks, preferred_element_type=jnp.float32
    ).astype(jnp.bfloat16)
    at_dst = at_dst.reshape(windows, -1, width)
    at_src = at_src.reshape(windows, -1, width)
    act_edge = (
        times_plain(edge_rows, edge_in[:width])
        + times_plain(at_dst, edge_in[width : 2 * width])
        + times_plain(at_src, edge_in[2 * width :])
    )
    hidden_edge = jax.nn.silu(act_edge).astype(jnp.bfloat16)
    edge_pre = times_plain(hidden_edge, edge_outer)
    message = normalize(edge_pre)[0]
    edge_new = (edge_rows.astype(jnp.float32) + message).astype(jnp.bfloat16)
    summed = exact_sum(
        "tkn,mtkd->mnd",
        dst_onehot.astype(jnp.float32),
        message.reshape(windows, tiles, edges_tile, width),
    ).astype(jnp.bfloat16)
    act_node = times_plain(node_blocks, node_in[:width]) + times_plain(summed, node_in[width:])
    hidden_node = jax.nn.silu(act_node).astype(jnp.bfloat16)
    node_pre = times_plain(hidden_node, node_outer)
    node_new = (node_blocks.astype(jnp.float32) + normalize(node_pre)[0]).astype(jnp.bfloat16)
    return (node_new, edge_new, (act_edge, edge_pre, act_node, node_pre))


def backward(weights, tables, kept_values, grad_node, grad_edge):
    edge_in, edge_outer, node_in, node_outer = weights
    dst_onehot, src_onehot, block_pick = tables
    act_edge, edge_pre, act_node, node_pre = kept_values
    windows, block_nodes, width = grad_node.shape
    tiles, edges_tile = dst_onehot.shape[:2]
    dst_float = dst_onehot.astype(jnp.float32)
    src_float = src_onehot.astype(jnp.float32)
    pre_node_grad = norm_back(node_pre, grad_node).astype(jnp.bfloat16)
    act_node_grad = (times_turned(pre_node_grad, node_outer) * silu_slope(act_node)).astype(
        jnp.bfloat16
    )
    node_self_grad = times_turned(act_node_grad, node_in[:width])
    summed_grad = times_turned(act_node_grad, node_in[width:])
    message_grad = grad_edge + exact_sum("tkn,mnd->mtkd", dst_float, summed_grad).reshape(
        windows, -1, width
    )
    pre_edge_grad = norm_back(edge_pre, message_grad).astype(jnp.bfloat16)
    act_edge_grad = (times_turned(pre_edge_grad, edge_outer) * silu_slope(act_edge)).astype(
        jnp.bfloat16
    )
    edge_self_grad = times_turned(act_edge_grad, edge_in[:width])
    dst_side_grad = times_turned(act_edge_grad, edge_in[width : 2 * width])
    src_side_grad = times_turned(act_edge_grad, edge_in[2 * width :])
    edge_back = grad_edge + edge_self_grad
    dst_sums = exact_sum(
        "tkn,mtkd->mnd", dst_float, dst_side_grad.reshape(windows, tiles, edges_tile, width)
    )
    per_tile = exact_sum(
        "tkn,mtkd->mtnd", src_float, src_side_grad.reshape(windows, tiles, edges_tile, width)
    )
    table_back = exact_sum("tb,mtnd->mbnd", block_pick, per_tile)
    node_back = grad_node + node_self_grad + dst_sums + return_to_owners(table_back)
    return (node_back, edge_back)


def body(
    node_latents,
    edge_latents,
    tile_offsets,
    edge_dst,
    edge_src,
    edge_in_w,
    edge_out_w,
    node_in_w,
    node_out_w,
    node_cot,
    edge_cot,
):
    windows = node_latents.shape[0]
    block_nodes = node_latents.shape[3]
    width = node_latents.shape[4]
    tile_codes = tile_offsets[0, 0]
    node_iota = lax.broadcasted_iota(jnp.int32, edge_dst[0, 0].shape + (block_nodes,), 2)
    dst_onehot = (edge_dst[0, 0][..., None] == node_iota).astype(jnp.bfloat16)
    src_onehot = (edge_src[0, 0][..., None] == node_iota).astype(jnp.bfloat16)
    block_iota = lax.broadcasted_iota(jnp.int32, tile_codes.shape + (9,), 1)
    block_pick = (tile_codes[..., None] == block_iota).astype(jnp.float32)
    tables = (dst_onehot, src_onehot, block_pick)
    is_first = lax.axis_index("phase") == 0
    own = jnp.concatenate([edge_in_w[0], edge_out_w[0], node_in_w[0], node_out_w[0]], axis=0)
    other = lax.ppermute(own, "phase", [(0, 1), (1, 0)])
    sections = (jnp.where(is_first, own, other), jnp.where(is_first, other, own))
    cuts = [0, 3 * width, 4 * width, 6 * width, 7 * width]
    weights = [
        tuple(packed[cuts[i] : cuts[i + 1]] for i in range(4)) for packed in sections
    ]
    node_zero = node_latents.reshape(windows, block_nodes, width)
    edge_zero = edge_latents.reshape(windows, -1, width)
    node_one, edge_one, kept_one = forward(weights[0], tables, node_zero, edge_zero)
    node_two, edge_two, kept_two = forward(weights[1], tables, node_one, edge_one)
    grad_node_one, grad_edge_one = backward(
        weights[1],
        tables,
        kept_two,
        node_cot.reshape(windows, block_nodes, width).astype(jnp.float32),
        edge_cot.reshape(windows, -1, width).astype(jnp.float32),
    )
    grad_node_zero, grad_edge_zero = backward(
        weights[0], tables, kept_one, grad_node_one, grad_edge_one
    )
    node_shape = (1,) + node_latents.shape
    edge_shape = (1,) + edge_latents.shape
    node_result = jnp.where(is_first, node_one, node_two).reshape(node_shape)
    edge_result = jnp.where(is_first, edge_one, edge_two).reshape(edge_shape)
    node_gradient = jnp.where(is_first, grad_node_zero, grad_node_one).reshape(node_shape)
    edge_gradient = jnp.where(is_first, grad_edge_zero, grad_edge_one).reshape(edge_shape)
    return (node_result, edge_result, node_gradient, edge_gradient)


def solution(mesh):
    return jax.shard_map(
        body,
        mesh=mesh,
        in_specs=(
            P(None, "px", "py", None, None),
            P(None, "px", "py", None, None, None),
            P("px", "py", None),
            P("px", "py", None, None),
            P("px", "py", None, None),
            P("phase", None, None),
            P("phase", None, None),
            P("phase", None, None),
            P("phase", None, None),
            P(None, "px", "py", None, None),
            P(None, "px", "py", None, None, None),
        ),
        out_specs=(
            P("phase", None, "px", "py", None, None),
            P("phase", None, "px", "py", None, None, None),
            P("phase", None, "px", "py", None, None),
            P("phase", None, "px", "py", None, None, None),
        ),
        check_vma=False,
    )
```

```python
import jax
import jax.numpy as jnp
from jax import lax
from jax.sharding import PartitionSpec as P


def shifted(array, axis, by):
    count = lax.axis_size(axis)
    pairs = [(i, i + by) for i in range(count) if 0 <= i + by < count]
    return lax.ppermute(array, axis, pairs)


def normalize(values):
    centred = values - jnp.mean(values, axis=-1, keepdims=True)
    inverse = lax.rsqrt(jnp.mean(centred * centred, axis=-1, keepdims=True) + 1e-05)
    return (centred * inverse, inverse)


def norm_back(values, upstream):
    normed, inverse = normalize(values)
    return inverse * (
        upstream
        - jnp.mean(upstream, axis=-1, keepdims=True)
        - normed * jnp.mean(upstream * normed, axis=-1, keepdims=True)
    )


def silu_slope(values):
    squash = jax.nn.sigmoid(values)
    return squash * (1.0 + values * (1.0 - squash))


def times_plain(left, right):
    return jnp.einsum("mrk,kd->mrd", left, right, preferred_element_type=jnp.float32)


def times_turned(left, right):
    return jnp.einsum("mrd,kd->mrk", left, right, preferred_element_type=jnp.float32)


def exact_sum(form, left, right):
    return jnp.einsum(
        form, left, right, precision=lax.Precision.HIGHEST, preferred_element_type=jnp.float32
    )


def neighbourhood(node_blocks):
    row = jnp.stack(
        [shifted(node_blocks, "py", 1), node_blocks, shifted(node_blocks, "py", -1)], axis=1
    )
    grid = jnp.stack([shifted(row, "px", 1), row, shifted(row, "px", -1)], axis=1)
    return grid.reshape((grid.shape[0], 9) + grid.shape[3:])


def return_to_owners(table_back):
    grid = table_back.reshape((table_back.shape[0], 3, 3) + table_back.shape[2:])
    low = grid[:, 0].astype(jnp.bfloat16)
    high = grid[:, 2].astype(jnp.bfloat16)
    row = (
        grid[:, 1]
        + shifted(low, "px", -1).astype(jnp.float32)
        + shifted(high, "px", 1).astype(jnp.float32)
    )
    low = row[:, 0].astype(jnp.bfloat16)
    high = row[:, 2].astype(jnp.bfloat16)
    return (
        row[:, 1]
        + shifted(low, "py", -1).astype(jnp.float32)
        + shifted(high, "py", 1).astype(jnp.float32)
    )


def forward(weights, tables, node_blocks, edge_rows):
    edge_in, edge_outer, node_in, node_outer = weights
    dst_onehot, src_onehot, block_pick = tables
    windows, block_nodes, width = node_blocks.shape
    tiles, edges_tile = dst_onehot.shape[:2]
    source_table = neighbourhood(node_blocks)
    at_dst = jnp.einsum(
        "tkn,mnd->mtkd", dst_onehot, node_blocks, preferred_element_type=jnp.float32
    ).astype(jnp.bfloat16)
    src_blocks = jnp.einsum(
        "tb,mbnd->mtnd", block_pick.astype(jnp.bfloat16), source_table,
        preferred_element_type=jnp.float32,
    ).astype(jnp.bfloat16)
    at_src = jnp.einsum(
        "tkn,mtnd->mtkd", src_onehot, src_blocks, preferred_element_type=jnp.float32
    ).astype(jnp.bfloat16)
    at_dst = at_dst.reshape(windows, -1, width)
    at_src = at_src.reshape(windows, -1, width)
    act_edge = (
        times_plain(edge_rows, edge_in[:width])
        + times_plain(at_dst, edge_in[width : 2 * width])
        + times_plain(at_src, edge_in[2 * width :])
    )
    hidden_edge = jax.nn.silu(act_edge).astype(jnp.bfloat16)
    edge_pre = times_plain(hidden_edge, edge_outer)
    message = normalize(edge_pre)[0]
    edge_new = (edge_rows.astype(jnp.float32) + message).astype(jnp.bfloat16)
    summed = exact_sum(
        "tkn,mtkd->mnd",
        dst_onehot.astype(jnp.float32),
        message.reshape(windows, tiles, edges_tile, width),
    ).astype(jnp.bfloat16)
    act_node = times_plain(node_blocks, node_in[:width]) + times_plain(summed, node_in[width:])
    hidden_node = jax.nn.silu(act_node).astype(jnp.bfloat16)
    node_pre = times_plain(hidden_node, node_outer)
    node_new = (node_blocks.astype(jnp.float32) + normalize(node_pre)[0]).astype(jnp.bfloat16)
    return (node_new, edge_new, (act_edge, edge_pre, act_node, node_pre))


def backward(weights, tables, kept_values, grad_node, grad_edge):
    edge_in, edge_outer, node_in, node_outer = weights
    dst_onehot, src_onehot, block_pick = tables
    act_edge, edge_pre, act_node, node_pre = kept_values
    windows, block_nodes, width = grad_node.shape
    tiles, edges_tile = dst_onehot.shape[:2]
    dst_float = dst_onehot.astype(jnp.float32)
    src_float = src_onehot.astype(jnp.float32)
    pre_node_grad = norm_back(node_pre, grad_node).astype(jnp.bfloat16)
    act_node_grad = (times_turned(pre_node_grad, node_outer) * silu_slope(act_node)).astype(
        jnp.bfloat16
    )
    node_self_grad = times_turned(act_node_grad, node_in[:width])
    summed_grad = times_turned(act_node_grad, node_in[width:])
    message_grad = grad_edge + exact_sum("tkn,mnd->mtkd", dst_float, summed_grad).reshape(
        windows, -1, width
    )
    pre_edge_grad = norm_back(edge_pre, message_grad).astype(jnp.bfloat16)
    act_edge_grad = (times_turned(pre_edge_grad, edge_outer) * silu_slope(act_edge)).astype(
        jnp.bfloat16
    )
    edge_self_grad = times_turned(act_edge_grad, edge_in[:width])
    dst_side_grad = times_turned(act_edge_grad, edge_in[width : 2 * width])
    src_side_grad = times_turned(act_edge_grad, edge_in[2 * width :])
    edge_back = grad_edge + edge_self_grad
    dst_sums = exact_sum(
        "tkn,mtkd->mnd", dst_float, dst_side_grad.reshape(windows, tiles, edges_tile, width)
    )
    per_tile = exact_sum(
        "tkn,mtkd->mtnd", src_float, src_side_grad.reshape(windows, tiles, edges_tile, width)
    )
    table_back = exact_sum("tb,mtnd->mbnd", block_pick, per_tile)
    node_back = grad_node + node_self_grad + dst_sums + return_to_owners(table_back)
    return (node_back, edge_back)


def body(
    node_latents,
    edge_latents,
    tile_offsets,
    edge_dst,
    edge_src,
    edge_in_w,
    edge_out_w,
    node_in_w,
    node_out_w,
    node_cot,
    edge_cot,
):
    windows = node_latents.shape[0]
    block_nodes = node_latents.shape[3]
    width = node_latents.shape[4]
    tile_codes = tile_offsets[0, 0]
    node_iota = lax.broadcasted_iota(jnp.int32, edge_dst[0, 0].shape + (block_nodes,), 2)
    dst_onehot = (edge_dst[0, 0][..., None] == node_iota).astype(jnp.bfloat16)
    src_onehot = (edge_src[0, 0][..., None] == node_iota).astype(jnp.bfloat16)
    block_iota = lax.broadcasted_iota(jnp.int32, tile_codes.shape + (9,), 1)
    block_pick = (tile_codes[..., None] == block_iota).astype(jnp.float32)
    tables = (dst_onehot, src_onehot, block_pick)
    is_first = lax.axis_index("phase") == 0
    own = jnp.concatenate([edge_in_w[0], edge_out_w[0], node_in_w[0], node_out_w[0]], axis=0)
    other = lax.ppermute(own, "phase", [(0, 1), (1, 0)])
    sections = (jnp.where(is_first, own, other), jnp.where(is_first, other, own))
    cuts = [0, 3 * width, 4 * width, 6 * width, 7 * width]
    weights = [
        tuple(packed[cuts[i] : cuts[i + 1]] for i in range(4)) for packed in sections
    ]
    def mine(array):
        return jnp.where(is_first, array[0], array[1])[None]

    node_zero = mine(node_latents).reshape(1, block_nodes, width)
    edge_zero = mine(edge_latents).reshape(1, -1, width)
    node_one, edge_one, kept_one = forward(weights[0], tables, node_zero, edge_zero)
    node_two, edge_two, kept_two = forward(weights[1], tables, node_one, edge_one)
    latent_send = jnp.where(
        is_first,
        jnp.concatenate([node_two[0], edge_two[0]], axis=0),
        jnp.concatenate([node_one[0], edge_one[0]], axis=0),
    )
    latent_recv = lax.ppermute(latent_send, "phase", [(0, 1), (1, 0)])
    grad_node_one, grad_edge_one = backward(
        weights[1],
        tables,
        kept_two,
        mine(node_cot).reshape(1, block_nodes, width).astype(jnp.float32),
        mine(edge_cot).reshape(1, -1, width).astype(jnp.float32),
    )
    grad_node_zero, grad_edge_zero = backward(
        weights[0], tables, kept_one, grad_node_one, grad_edge_one
    )
    grad_send = jnp.where(
        is_first,
        jnp.concatenate([grad_node_one[0], grad_edge_one[0]], axis=0),
        jnp.concatenate([grad_node_zero[0], grad_edge_zero[0]], axis=0),
    )
    grad_recv = lax.ppermute(grad_send, "phase", [(0, 1), (1, 0)])

    def placed(own_first, own_second, received, shape):
        kept = jnp.where(is_first, own_first, own_second)
        pair = jnp.where(
            is_first, jnp.stack([kept, received]), jnp.stack([received, kept])
        )
        return pair.reshape(shape)

    node_shape = (1,) + node_latents.shape
    edge_shape = (1,) + edge_latents.shape
    node_result = placed(node_one[0], node_two[0], latent_recv[:block_nodes], node_shape)
    edge_result = placed(edge_one[0], edge_two[0], latent_recv[block_nodes:], edge_shape)
    node_gradient = placed(
        grad_node_zero[0], grad_node_one[0], grad_recv[:block_nodes], node_shape
    )
    edge_gradient = placed(
        grad_edge_zero[0], grad_edge_one[0], grad_recv[block_nodes:], edge_shape
    )
    return (node_result, edge_result, node_gradient, edge_gradient)


def solution(mesh):
    return jax.shard_map(
        body,
        mesh=mesh,
        in_specs=(
            P(None, "px", "py", None, None),
            P(None, "px", "py", None, None, None),
            P("px", "py", None),
            P("px", "py", None, None),
            P("px", "py", None, None),
            P("phase", None, None),
            P("phase", None, None),
            P("phase", None, None),
            P("phase", None, None),
            P(None, "px", "py", None, None),
            P(None, "px", "py", None, None, None),
        ),
        out_specs=(
            P("phase", None, "px", "py", None, None),
            P("phase", None, "px", "py", None, None, None),
            P("phase", None, "px", "py", None, None),
            P("phase", None, "px", "py", None, None, None),
        ),
        check_vma=False,
    )
```

```python
import jax
import jax.numpy as jnp
from jax import lax
from jax.sharding import PartitionSpec as P


def normalize(values):
    centred = values - jnp.mean(values, axis=-1, keepdims=True)
    inverse = lax.rsqrt(jnp.mean(centred * centred, axis=-1, keepdims=True) + 1e-05)
    return (centred * inverse, inverse)


def norm_back(values, upstream):
    normed, inverse = normalize(values)
    return inverse * (
        upstream
        - jnp.mean(upstream, axis=-1, keepdims=True)
        - normed * jnp.mean(upstream * normed, axis=-1, keepdims=True)
    )


def silu_slope(values):
    squash = jax.nn.sigmoid(values)
    return squash * (1.0 + values * (1.0 - squash))


def times_plain(left, right):
    return jnp.einsum("mrk,kd->mrd", left, right, preferred_element_type=jnp.float32)


def times_turned(left, right):
    return jnp.einsum("mrd,kd->mrk", left, right, preferred_element_type=jnp.float32)


def exact_sum(form, left, right):
    return jnp.einsum(
        form, left, right, precision=lax.Precision.HIGHEST, preferred_element_type=jnp.float32
    )


OFFSETS = [(dx, dy) for dx in (-1, 0, 1) for dy in (-1, 0, 1)]


def from_offset(array, dx, dy):
    rows = lax.axis_size("px")
    cols = lax.axis_size("py")
    pairs = [
        ((i + dx) * cols + j + dy, i * cols + j)
        for i in range(rows)
        for j in range(cols)
        if 0 <= i + dx < rows and 0 <= j + dy < cols
    ]
    return lax.ppermute(array, ("px", "py"), pairs)


def neighbourhood(node_blocks):
    parts = [
        node_blocks if (dx, dy) == (0, 0) else from_offset(node_blocks, dx, dy)
        for dx, dy in OFFSETS
    ]
    return jnp.stack(parts, axis=1)


def return_to_owners(table_back):
    total = table_back[:, 4]
    for index, (dx, dy) in enumerate(OFFSETS):
        if (dx, dy) != (0, 0):
            sent = table_back[:, index].astype(jnp.bfloat16)
            total = total + from_offset(sent, -dx, -dy).astype(jnp.float32)
    return total


def forward(weights, tables, node_blocks, edge_rows):
    edge_in, edge_outer, node_in, node_outer = weights
    dst_onehot, src_onehot, block_pick = tables
    windows, block_nodes, width = node_blocks.shape
    tiles, edges_tile = dst_onehot.shape[:2]
    source_table = neighbourhood(node_blocks)
    at_dst = jnp.einsum(
        "tkn,mnd->mtkd", dst_onehot, node_blocks, preferred_element_type=jnp.float32
    ).astype(jnp.bfloat16)
    src_blocks = jnp.einsum(
        "tb,mbnd->mtnd", block_pick.astype(jnp.bfloat16), source_table,
        preferred_element_type=jnp.float32,
    ).astype(jnp.bfloat16)
    at_src = jnp.einsum(
        "tkn,mtnd->mtkd", src_onehot, src_blocks, preferred_element_type=jnp.float32
    ).astype(jnp.bfloat16)
    at_dst = at_dst.reshape(windows, -1, width)
    at_src = at_src.reshape(windows, -1, width)
    act_edge = (
        times_plain(edge_rows, edge_in[:width])
        + times_plain(at_dst, edge_in[width : 2 * width])
        + times_plain(at_src, edge_in[2 * width :])
    )
    hidden_edge = jax.nn.silu(act_edge).astype(jnp.bfloat16)
    edge_pre = times_plain(hidden_edge, edge_outer)
    message = normalize(edge_pre)[0]
    edge_new = (edge_rows.astype(jnp.float32) + message).astype(jnp.bfloat16)
    summed = exact_sum(
        "tkn,mtkd->mnd",
        dst_onehot.astype(jnp.float32),
        message.reshape(windows, tiles, edges_tile, width),
    ).astype(jnp.bfloat16)
    act_node = times_plain(node_blocks, node_in[:width]) + times_plain(summed, node_in[width:])
    hidden_node = jax.nn.silu(act_node).astype(jnp.bfloat16)
    node_pre = times_plain(hidden_node, node_outer)
    node_new = (node_blocks.astype(jnp.float32) + normalize(node_pre)[0]).astype(jnp.bfloat16)
    return (node_new, edge_new, (act_edge, edge_pre, act_node, node_pre))


def backward(weights, tables, kept_values, grad_node, grad_edge):
    edge_in, edge_outer, node_in, node_outer = weights
    dst_onehot, src_onehot, block_pick = tables
    act_edge, edge_pre, act_node, node_pre = kept_values
    windows, block_nodes, width = grad_node.shape
    tiles, edges_tile = dst_onehot.shape[:2]
    dst_float = dst_onehot.astype(jnp.float32)
    src_float = src_onehot.astype(jnp.float32)
    pre_node_grad = norm_back(node_pre, grad_node).astype(jnp.bfloat16)
    act_node_grad = (times_turned(pre_node_grad, node_outer) * silu_slope(act_node)).astype(
        jnp.bfloat16
    )
    node_self_grad = times_turned(act_node_grad, node_in[:width])
    summed_grad = times_turned(act_node_grad, node_in[width:])
    message_grad = grad_edge + exact_sum("tkn,mnd->mtkd", dst_float, summed_grad).reshape(
        windows, -1, width
    )
    pre_edge_grad = norm_back(edge_pre, message_grad).astype(jnp.bfloat16)
    act_edge_grad = (times_turned(pre_edge_grad, edge_outer) * silu_slope(act_edge)).astype(
        jnp.bfloat16
    )
    edge_self_grad = times_turned(act_edge_grad, edge_in[:width])
    dst_side_grad = times_turned(act_edge_grad, edge_in[width : 2 * width])
    src_side_grad = times_turned(act_edge_grad, edge_in[2 * width :])
    edge_back = grad_edge + edge_self_grad
    dst_sums = exact_sum(
        "tkn,mtkd->mnd", dst_float, dst_side_grad.reshape(windows, tiles, edges_tile, width)
    )
    per_tile = exact_sum(
        "tkn,mtkd->mtnd", src_float, src_side_grad.reshape(windows, tiles, edges_tile, width)
    )
    table_back = exact_sum("tb,mtnd->mbnd", block_pick, per_tile)
    node_back = grad_node + node_self_grad + dst_sums + return_to_owners(table_back)
    return (node_back, edge_back)


def body(
    node_latents,
    edge_latents,
    tile_offsets,
    edge_dst,
    edge_src,
    edge_in_w,
    edge_out_w,
    node_in_w,
    node_out_w,
    node_cot,
    edge_cot,
):
    windows = node_latents.shape[0]
    block_nodes = node_latents.shape[3]
    width = node_latents.shape[4]
    tile_codes = tile_offsets[0, 0]
    node_iota = lax.broadcasted_iota(jnp.int32, edge_dst[0, 0].shape + (block_nodes,), 2)
    dst_onehot = (edge_dst[0, 0][..., None] == node_iota).astype(jnp.bfloat16)
    src_onehot = (edge_src[0, 0][..., None] == node_iota).astype(jnp.bfloat16)
    block_iota = lax.broadcasted_iota(jnp.int32, tile_codes.shape + (9,), 1)
    block_pick = (tile_codes[..., None] == block_iota).astype(jnp.float32)
    tables = (dst_onehot, src_onehot, block_pick)
    is_first = lax.axis_index("phase") == 0
    own = jnp.concatenate([edge_in_w[0], edge_out_w[0], node_in_w[0], node_out_w[0]], axis=0)
    other = lax.ppermute(own, "phase", [(0, 1), (1, 0)])
    sections = (jnp.where(is_first, own, other), jnp.where(is_first, other, own))
    cuts = [0, 3 * width, 4 * width, 6 * width, 7 * width]
    weights = [
        tuple(packed[cuts[i] : cuts[i + 1]] for i in range(4)) for packed in sections
    ]
    def mine(array):
        return jnp.where(is_first, array[0], array[1])[None]

    node_zero = mine(node_latents).reshape(1, block_nodes, width)
    edge_zero = mine(edge_latents).reshape(1, -1, width)
    node_one, edge_one, kept_one = forward(weights[0], tables, node_zero, edge_zero)
    node_two, edge_two, kept_two = forward(weights[1], tables, node_one, edge_one)
    latent_send = jnp.where(
        is_first,
        jnp.concatenate([node_two[0], edge_two[0]], axis=0),
        jnp.concatenate([node_one[0], edge_one[0]], axis=0),
    )
    latent_recv = lax.ppermute(latent_send, "phase", [(0, 1), (1, 0)])
    grad_node_one, grad_edge_one = backward(
        weights[1],
        tables,
        kept_two,
        mine(node_cot).reshape(1, block_nodes, width).astype(jnp.float32),
        mine(edge_cot).reshape(1, -1, width).astype(jnp.float32),
    )
    grad_node_zero, grad_edge_zero = backward(
        weights[0], tables, kept_one, grad_node_one, grad_edge_one
    )
    grad_send = jnp.where(
        is_first,
        jnp.concatenate([grad_node_one[0], grad_edge_one[0]], axis=0),
        jnp.concatenate([grad_node_zero[0], grad_edge_zero[0]], axis=0),
    )
    grad_recv = lax.ppermute(grad_send, "phase", [(0, 1), (1, 0)])

    def placed(own_first, own_second, received, shape):
        kept = jnp.where(is_first, own_first, own_second)
        pair = jnp.where(
            is_first, jnp.stack([kept, received]), jnp.stack([received, kept])
        )
        return pair.reshape(shape)

    node_shape = (1,) + node_latents.shape
    edge_shape = (1,) + edge_latents.shape
    node_result = placed(node_one[0], node_two[0], latent_recv[:block_nodes], node_shape)
    edge_result = placed(edge_one[0], edge_two[0], latent_recv[block_nodes:], edge_shape)
    node_gradient = placed(
        grad_node_zero[0], grad_node_one[0], grad_recv[:block_nodes], node_shape
    )
    edge_gradient = placed(
        grad_edge_zero[0], grad_edge_one[0], grad_recv[block_nodes:], edge_shape
    )
    return (node_result, edge_result, node_gradient, edge_gradient)


def solution(mesh):
    return jax.shard_map(
        body,
        mesh=mesh,
        in_specs=(
            P(None, "px", "py", None, None),
            P(None, "px", "py", None, None, None),
            P("px", "py", None),
            P("px", "py", None, None),
            P("px", "py", None, None),
            P("phase", None, None),
            P("phase", None, None),
            P("phase", None, None),
            P("phase", None, None),
            P(None, "px", "py", None, None),
            P(None, "px", "py", None, None, None),
        ),
        out_specs=(
            P("phase", None, "px", "py", None, None),
            P("phase", None, "px", "py", None, None, None),
            P("phase", None, "px", "py", None, None),
            P("phase", None, "px", "py", None, None, None),
        ),
        check_vma=False,
    )
```

```python
import jax
import jax.numpy as jnp
from jax import lax
from jax.sharding import PartitionSpec as P


def shifted(array, axis, by):
    count = lax.axis_size(axis)
    pairs = [(i, i + by) for i in range(count) if 0 <= i + by < count]
    return lax.ppermute(array, axis, pairs)


def normalize(values):
    centred = values - jnp.mean(values, axis=-1, keepdims=True)
    inverse = lax.rsqrt(jnp.mean(centred * centred, axis=-1, keepdims=True) + 1e-05)
    return (centred * inverse, inverse)


def norm_back(values, upstream):
    normed, inverse = normalize(values)
    return inverse * (
        upstream
        - jnp.mean(upstream, axis=-1, keepdims=True)
        - normed * jnp.mean(upstream * normed, axis=-1, keepdims=True)
    )


def silu_slope(values):
    squash = jax.nn.sigmoid(values)
    return squash * (1.0 + values * (1.0 - squash))


def times_plain(left, right):
    return jnp.einsum("mrk,kd->mrd", left, right, preferred_element_type=jnp.float32)


def times_turned(left, right):
    return jnp.einsum("mrd,kd->mrk", left, right, preferred_element_type=jnp.float32)


def onehot_sum(form, left, right):
    return jnp.einsum(
        form, left, right, precision=lax.Precision.HIGH, preferred_element_type=jnp.float32
    )


def neighbourhood(node_blocks):
    row = jnp.stack(
        [shifted(node_blocks, "py", 1), node_blocks, shifted(node_blocks, "py", -1)], axis=1
    )
    grid = jnp.stack([shifted(row, "px", 1), row, shifted(row, "px", -1)], axis=1)
    return grid.reshape((grid.shape[0], 9) + grid.shape[3:])


def return_to_owners(table_back):
    grid = table_back.reshape((table_back.shape[0], 3, 3) + table_back.shape[2:])
    low = grid[:, 0].astype(jnp.bfloat16)
    high = grid[:, 2].astype(jnp.bfloat16)
    row = (
        grid[:, 1]
        + shifted(low, "px", -1).astype(jnp.float32)
        + shifted(high, "px", 1).astype(jnp.float32)
    )
    low = row[:, 0].astype(jnp.bfloat16)
    high = row[:, 2].astype(jnp.bfloat16)
    return (
        row[:, 1]
        + shifted(low, "py", -1).astype(jnp.float32)
        + shifted(high, "py", 1).astype(jnp.float32)
    )


def forward(weights, tables, node_blocks, edge_rows):
    edge_in, edge_outer, node_in, node_outer = weights
    dst_onehot, src_onehot = tables
    windows, block_nodes, width = node_blocks.shape
    source_table = neighbourhood(node_blocks).reshape(windows, -1, width)
    at_dst = jnp.einsum(
        "en,mnd->med", dst_onehot, node_blocks, preferred_element_type=jnp.float32
    ).astype(jnp.bfloat16)
    at_src = jnp.einsum(
        "en,mnd->med", src_onehot, source_table, preferred_element_type=jnp.float32
    ).astype(jnp.bfloat16)
    joined = jnp.concatenate([edge_rows, at_dst, at_src], axis=2)
    act_edge = times_plain(joined, edge_in)
    hidden_edge = jax.nn.silu(act_edge).astype(jnp.bfloat16)
    edge_pre = times_plain(hidden_edge, edge_outer)
    message = normalize(edge_pre)[0]
    edge_new = (edge_rows.astype(jnp.float32) + message).astype(jnp.bfloat16)
    summed = onehot_sum("en,med->mnd", dst_onehot, message).astype(jnp.bfloat16)
    node_joined = jnp.concatenate([node_blocks, summed], axis=2)
    act_node = times_plain(node_joined, node_in)
    hidden_node = jax.nn.silu(act_node).astype(jnp.bfloat16)
    node_pre = times_plain(hidden_node, node_outer)
    node_new = (node_blocks.astype(jnp.float32) + normalize(node_pre)[0]).astype(jnp.bfloat16)
    return (node_new, edge_new, (act_edge, edge_pre, act_node, node_pre))


def backward(weights, tables, kept_values, grad_node, grad_edge):
    edge_in, edge_outer, node_in, node_outer = weights
    dst_onehot, src_onehot = tables
    act_edge, edge_pre, act_node, node_pre = kept_values
    windows, block_nodes, width = grad_node.shape
    pre_node_grad = norm_back(node_pre, grad_node).astype(jnp.bfloat16)
    act_node_grad = (times_turned(pre_node_grad, node_outer) * silu_slope(act_node)).astype(
        jnp.bfloat16
    )
    joined_node_grad = times_turned(act_node_grad, node_in)
    message_grad = grad_edge + onehot_sum("en,mnd->med", dst_onehot, joined_node_grad[:, :, width:])
    pre_edge_grad = norm_back(edge_pre, message_grad).astype(jnp.bfloat16)
    act_edge_grad = (times_turned(pre_edge_grad, edge_outer) * silu_slope(act_edge)).astype(
        jnp.bfloat16
    )
    joined_edge_grad = times_turned(act_edge_grad, edge_in)
    edge_back = grad_edge + joined_edge_grad[:, :, :width]
    dst_sums = onehot_sum("en,med->mnd", dst_onehot, joined_edge_grad[:, :, width : 2 * width])
    table_back = onehot_sum("en,med->mnd", src_onehot, joined_edge_grad[:, :, 2 * width :])
    table_back = table_back.reshape(windows, 9, block_nodes, width)
    node_back = (
        grad_node + joined_node_grad[:, :, :width] + dst_sums + return_to_owners(table_back)
    )
    return (node_back, edge_back)


def body(
    node_latents,
    edge_latents,
    tile_offsets,
    edge_dst,
    edge_src,
    edge_in_w,
    edge_out_w,
    node_in_w,
    node_out_w,
    node_cot,
    edge_cot,
):
    windows = node_latents.shape[0]
    block_nodes = node_latents.shape[3]
    width = node_latents.shape[4]
    tile_codes = tile_offsets[0, 0]
    tiles, edges_tile = edge_dst.shape[2:]
    node_iota = lax.broadcasted_iota(jnp.int32, (tiles * edges_tile, block_nodes), 1)
    dst_onehot = (edge_dst.reshape(-1, 1) == node_iota).astype(jnp.bfloat16)
    source_key = (tile_codes[:, None] * block_nodes + edge_src[0, 0]).reshape(-1, 1)
    table_iota = lax.broadcasted_iota(jnp.int32, (tiles * edges_tile, 9 * block_nodes), 1)
    src_onehot = (source_key == table_iota).astype(jnp.bfloat16)
    tables = (dst_onehot, src_onehot)
    is_first = lax.axis_index("phase") == 0
    own = jnp.concatenate([edge_in_w[0], edge_out_w[0], node_in_w[0], node_out_w[0]], axis=0)
    other = lax.ppermute(own, "phase", [(0, 1), (1, 0)])
    sections = (jnp.where(is_first, own, other), jnp.where(is_first, other, own))
    cuts = [0, 3 * width, 4 * width, 6 * width, 7 * width]
    weights = [
        tuple(packed[cuts[i] : cuts[i + 1]] for i in range(4)) for packed in sections
    ]
    def mine(array):
        return jnp.where(is_first, array[0], array[1])[None]

    node_zero = mine(node_latents).reshape(1, block_nodes, width)
    edge_zero = mine(edge_latents).reshape(1, -1, width)
    node_one, edge_one, kept_one = forward(weights[0], tables, node_zero, edge_zero)
    node_two, edge_two, kept_two = forward(weights[1], tables, node_one, edge_one)
    latent_send = jnp.where(
        is_first,
        jnp.concatenate([node_two[0], edge_two[0]], axis=0),
        jnp.concatenate([node_one[0], edge_one[0]], axis=0),
    )
    latent_recv = lax.ppermute(latent_send, "phase", [(0, 1), (1, 0)])
    grad_node_one, grad_edge_one = backward(
        weights[1],
        tables,
        kept_two,
        mine(node_cot).reshape(1, block_nodes, width).astype(jnp.float32),
        mine(edge_cot).reshape(1, -1, width).astype(jnp.float32),
    )
    grad_node_zero, grad_edge_zero = backward(
        weights[0], tables, kept_one, grad_node_one, grad_edge_one
    )
    grad_send = jnp.where(
        is_first,
        jnp.concatenate([grad_node_one[0], grad_edge_one[0]], axis=0),
        jnp.concatenate([grad_node_zero[0], grad_edge_zero[0]], axis=0),
    )
    grad_recv = lax.ppermute(grad_send, "phase", [(0, 1), (1, 0)])

    def placed(own_first, own_second, received, shape):
        kept = jnp.where(is_first, own_first, own_second)
        pair = jnp.where(
            is_first, jnp.stack([kept, received]), jnp.stack([received, kept])
        )
        return pair.reshape(shape)

    node_shape = (1,) + node_latents.shape
    edge_shape = (1,) + edge_latents.shape
    node_result = placed(node_one[0], node_two[0], latent_recv[:block_nodes], node_shape)
    edge_result = placed(edge_one[0], edge_two[0], latent_recv[block_nodes:], edge_shape)
    node_gradient = placed(
        grad_node_zero[0], grad_node_one[0], grad_recv[:block_nodes], node_shape
    )
    edge_gradient = placed(
        grad_edge_zero[0], grad_edge_one[0], grad_recv[block_nodes:], edge_shape
    )
    return (node_result, edge_result, node_gradient, edge_gradient)


def solution(mesh):
    return jax.shard_map(
        body,
        mesh=mesh,
        in_specs=(
            P(None, "px", "py", None, None),
            P(None, "px", "py", None, None, None),
            P("px", "py", None),
            P("px", "py", None, None),
            P("px", "py", None, None),
            P("phase", None, None),
            P("phase", None, None),
            P("phase", None, None),
            P("phase", None, None),
            P(None, "px", "py", None, None),
            P(None, "px", "py", None, None, None),
        ),
        out_specs=(
            P("phase", None, "px", "py", None, None),
            P("phase", None, "px", "py", None, None, None),
            P("phase", None, "px", "py", None, None),
            P("phase", None, "px", "py", None, None, None),
        ),
        check_vma=False,
    )
```

```python
import jax
import jax.numpy as jnp
from jax import lax
from jax.sharding import PartitionSpec as P


def shifted(array, axis, by):
    count = lax.axis_size(axis)
    pairs = [(i, i + by) for i in range(count) if 0 <= i + by < count]
    return lax.ppermute(array, axis, pairs)


def normalize(values):
    centred = values - jnp.mean(values, axis=-1, keepdims=True)
    inverse = lax.rsqrt(jnp.mean(centred * centred, axis=-1, keepdims=True) + 1e-05)
    return (centred * inverse, inverse)


def norm_back(values, upstream):
    normed, inverse = normalize(values)
    return inverse * (
        upstream
        - jnp.mean(upstream, axis=-1, keepdims=True)
        - normed * jnp.mean(upstream * normed, axis=-1, keepdims=True)
    )


def silu_slope(values):
    squash = jax.nn.sigmoid(values)
    return squash * (1.0 + values * (1.0 - squash))


def times_plain(left, right):
    return jnp.einsum("mrk,kd->mrd", left, right, preferred_element_type=jnp.float32)


def times_turned(left, right):
    return jnp.einsum("mrd,kd->mrk", left, right, preferred_element_type=jnp.float32)


def onehot_sum(form, left, right):
    high = right.astype(jnp.bfloat16)
    low = (right - high.astype(jnp.float32)).astype(jnp.bfloat16)
    both = jnp.einsum(
        form, left, jnp.concatenate([high, low], axis=-1), preferred_element_type=jnp.float32
    )
    width = right.shape[-1]
    return both[..., :width] + both[..., width:]


def neighbourhood(node_blocks):
    row = jnp.stack(
        [shifted(node_blocks, "py", 1), node_blocks, shifted(node_blocks, "py", -1)], axis=1
    )
    grid = jnp.stack([shifted(row, "px", 1), row, shifted(row, "px", -1)], axis=1)
    return grid.reshape((grid.shape[0], 9) + grid.shape[3:])


def return_to_owners(table_back):
    grid = table_back.reshape((table_back.shape[0], 3, 3) + table_back.shape[2:])
    low = grid[:, 0].astype(jnp.bfloat16)
    high = grid[:, 2].astype(jnp.bfloat16)
    row = (
        grid[:, 1]
        + shifted(low, "px", -1).astype(jnp.float32)
        + shifted(high, "px", 1).astype(jnp.float32)
    )
    low = row[:, 0].astype(jnp.bfloat16)
    high = row[:, 2].astype(jnp.bfloat16)
    return (
        row[:, 1]
        + shifted(low, "py", -1).astype(jnp.float32)
        + shifted(high, "py", 1).astype(jnp.float32)
    )


def forward(weights, tables, node_blocks, edge_rows):
    edge_in, edge_outer, node_in, node_outer = weights
    dst_onehot, src_onehot = tables
    windows, block_nodes, width = node_blocks.shape
    source_table = neighbourhood(node_blocks).reshape(windows, -1, width)
    at_dst = jnp.einsum(
        "en,mnd->med", dst_onehot, node_blocks, preferred_element_type=jnp.float32
    ).astype(jnp.bfloat16)
    at_src = jnp.einsum(
        "en,mnd->med", src_onehot, source_table, preferred_element_type=jnp.float32
    ).astype(jnp.bfloat16)
    joined = jnp.concatenate([edge_rows, at_dst, at_src], axis=2)
    act_edge = times_plain(joined, edge_in)
    hidden_edge = jax.nn.silu(act_edge).astype(jnp.bfloat16)
    edge_pre = times_plain(hidden_edge, edge_outer)
    message = normalize(edge_pre)[0]
    edge_new = (edge_rows.astype(jnp.float32) + message).astype(jnp.bfloat16)
    summed = onehot_sum("en,med->mnd", dst_onehot, message).astype(jnp.bfloat16)
    node_joined = jnp.concatenate([node_blocks, summed], axis=2)
    act_node = times_plain(node_joined, node_in)
    hidden_node = jax.nn.silu(act_node).astype(jnp.bfloat16)
    node_pre = times_plain(hidden_node, node_outer)
    node_new = (node_blocks.astype(jnp.float32) + normalize(node_pre)[0]).astype(jnp.bfloat16)
    return (node_new, edge_new, (act_edge, edge_pre, act_node, node_pre))


def backward(weights, tables, kept_values, grad_node, grad_edge):
    edge_in, edge_outer, node_in, node_outer = weights
    dst_onehot, src_onehot = tables
    act_edge, edge_pre, act_node, node_pre = kept_values
    windows, block_nodes, width = grad_node.shape
    pre_node_grad = norm_back(node_pre, grad_node).astype(jnp.bfloat16)
    act_node_grad = (times_turned(pre_node_grad, node_outer) * silu_slope(act_node)).astype(
        jnp.bfloat16
    )
    joined_node_grad = times_turned(act_node_grad, node_in)
    message_grad = grad_edge + onehot_sum("en,mnd->med", dst_onehot, joined_node_grad[:, :, width:])
    pre_edge_grad = norm_back(edge_pre, message_grad).astype(jnp.bfloat16)
    act_edge_grad = (times_turned(pre_edge_grad, edge_outer) * silu_slope(act_edge)).astype(
        jnp.bfloat16
    )
    joined_edge_grad = times_turned(act_edge_grad, edge_in)
    edge_back = grad_edge + joined_edge_grad[:, :, :width]
    dst_sums = onehot_sum("en,med->mnd", dst_onehot, joined_edge_grad[:, :, width : 2 * width])
    table_back = onehot_sum("en,med->mnd", src_onehot, joined_edge_grad[:, :, 2 * width :])
    table_back = table_back.reshape(windows, 9, block_nodes, width)
    node_back = (
        grad_node + joined_node_grad[:, :, :width] + dst_sums + return_to_owners(table_back)
    )
    return (node_back, edge_back)


def body(
    node_latents,
    edge_latents,
    tile_offsets,
    edge_dst,
    edge_src,
    edge_in_w,
    edge_out_w,
    node_in_w,
    node_out_w,
    node_cot,
    edge_cot,
):
    windows = node_latents.shape[0]
    block_nodes = node_latents.shape[3]
    width = node_latents.shape[4]
    tile_codes = tile_offsets[0, 0]
    tiles, edges_tile = edge_dst.shape[2:]
    node_iota = lax.broadcasted_iota(jnp.int32, (tiles * edges_tile, block_nodes), 1)
    dst_onehot = (edge_dst.reshape(-1, 1) == node_iota).astype(jnp.bfloat16)
    source_key = (tile_codes[:, None] * block_nodes + edge_src[0, 0]).reshape(-1, 1)
    table_iota = lax.broadcasted_iota(jnp.int32, (tiles * edges_tile, 9 * block_nodes), 1)
    src_onehot = (source_key == table_iota).astype(jnp.bfloat16)
    tables = (dst_onehot, src_onehot)
    is_first = lax.axis_index("phase") == 0
    own = jnp.concatenate([edge_in_w[0], edge_out_w[0], node_in_w[0], node_out_w[0]], axis=0)
    other = lax.ppermute(own, "phase", [(0, 1), (1, 0)])
    sections = (jnp.where(is_first, own, other), jnp.where(is_first, other, own))
    cuts = [0, 3 * width, 4 * width, 6 * width, 7 * width]
    weights = [
        tuple(packed[cuts[i] : cuts[i + 1]] for i in range(4)) for packed in sections
    ]
    def mine(array):
        return lax.dynamic_slice_in_dim(array, lax.axis_index("phase"), 1, axis=0)

    node_zero = mine(node_latents).reshape(1, block_nodes, width)
    edge_zero = mine(edge_latents).reshape(1, -1, width)
    node_one, edge_one, kept_one = forward(weights[0], tables, node_zero, edge_zero)
    node_two, edge_two, kept_two = forward(weights[1], tables, node_one, edge_one)
    latent_send = jnp.where(
        is_first,
        jnp.concatenate([node_two[0], edge_two[0]], axis=0),
        jnp.concatenate([node_one[0], edge_one[0]], axis=0),
    )
    latent_recv = lax.ppermute(latent_send, "phase", [(0, 1), (1, 0)])
    grad_node_one, grad_edge_one = backward(
        weights[1],
        tables,
        kept_two,
        mine(node_cot).reshape(1, block_nodes, width).astype(jnp.float32),
        mine(edge_cot).reshape(1, -1, width).astype(jnp.float32),
    )
    grad_node_zero, grad_edge_zero = backward(
        weights[0], tables, kept_one, grad_node_one, grad_edge_one
    )
    grad_send = jnp.where(
        is_first,
        jnp.concatenate([grad_node_one[0], grad_edge_one[0]], axis=0),
        jnp.concatenate([grad_node_zero[0], grad_edge_zero[0]], axis=0),
    )
    grad_recv = lax.ppermute(grad_send, "phase", [(0, 1), (1, 0)])

    def placed(own_first, own_second, received, shape):
        first = jnp.where(is_first, own_first, received)
        second = jnp.where(is_first, received, own_second)
        return jnp.stack([first, second]).reshape(shape)

    node_shape = (1,) + node_latents.shape
    edge_shape = (1,) + edge_latents.shape
    node_result = placed(node_one[0], node_two[0], latent_recv[:block_nodes], node_shape)
    edge_result = placed(edge_one[0], edge_two[0], latent_recv[block_nodes:], edge_shape)
    node_gradient = placed(
        grad_node_zero[0], grad_node_one[0], grad_recv[:block_nodes], node_shape
    )
    edge_gradient = placed(
        grad_edge_zero[0], grad_edge_one[0], grad_recv[block_nodes:], edge_shape
    )
    return (node_result, edge_result, node_gradient, edge_gradient)


def solution(mesh):
    return jax.shard_map(
        body,
        mesh=mesh,
        in_specs=(
            P(None, "px", "py", None, None),
            P(None, "px", "py", None, None, None),
            P("px", "py", None),
            P("px", "py", None, None),
            P("px", "py", None, None),
            P("phase", None, None),
            P("phase", None, None),
            P("phase", None, None),
            P("phase", None, None),
            P(None, "px", "py", None, None),
            P(None, "px", "py", None, None, None),
        ),
        out_specs=(
            P("phase", None, "px", "py", None, None),
            P("phase", None, "px", "py", None, None, None),
            P("phase", None, "px", "py", None, None),
            P("phase", None, "px", "py", None, None, None),
        ),
        check_vma=False,
    )
```

```python
import jax
import jax.numpy as jnp
from jax import lax
from jax.sharding import PartitionSpec as P


def shifted(array, axis, by):
    count = lax.axis_size(axis)
    pairs = [(i, i + by) for i in range(count) if 0 <= i + by < count]
    return lax.ppermute(array, axis, pairs)


def normalize(values):
    centred = values - jnp.mean(values, axis=-1, keepdims=True)
    inverse = lax.rsqrt(jnp.mean(centred * centred, axis=-1, keepdims=True) + 1e-05)
    return (centred * inverse, inverse)


def norm_back(values, upstream):
    normed, inverse = normalize(values)
    return inverse * (
        upstream
        - jnp.mean(upstream, axis=-1, keepdims=True)
        - normed * jnp.mean(upstream * normed, axis=-1, keepdims=True)
    )


def silu_slope(values):
    squash = jax.nn.sigmoid(values)
    return squash * (1.0 + values * (1.0 - squash))


def times_plain(left, right):
    return jnp.einsum("mrk,kd->mrd", left, right, preferred_element_type=jnp.float32)


def times_turned(left, right):
    return jnp.einsum("mrd,kd->mrk", left, right, preferred_element_type=jnp.float32)


def onehot_sum(form, left, right):
    return jnp.einsum(
        form, left, right, precision=lax.Precision.HIGH, preferred_element_type=jnp.float32
    )


def neighbourhood(node_blocks):
    row = jnp.stack(
        [shifted(node_blocks, "py", 1), node_blocks, shifted(node_blocks, "py", -1)], axis=1
    )
    grid = jnp.stack([shifted(row, "px", 1), row, shifted(row, "px", -1)], axis=1)
    return grid.reshape((grid.shape[0], 9) + grid.shape[3:])


def return_to_owners(table_back):
    grid = table_back.reshape((table_back.shape[0], 3, 3) + table_back.shape[2:])
    low = grid[:, 0].astype(jnp.bfloat16)
    high = grid[:, 2].astype(jnp.bfloat16)
    row = (
        grid[:, 1]
        + shifted(low, "px", -1).astype(jnp.float32)
        + shifted(high, "px", 1).astype(jnp.float32)
    )
    low = row[:, 0].astype(jnp.bfloat16)
    high = row[:, 2].astype(jnp.bfloat16)
    return (
        row[:, 1]
        + shifted(low, "py", -1).astype(jnp.float32)
        + shifted(high, "py", 1).astype(jnp.float32)
    )


def forward(weights, tables, node_blocks, edge_rows):
    edge_in, edge_outer, node_in, node_outer = weights
    dst_onehot, src_onehot = tables
    windows, block_nodes, width = node_blocks.shape
    source_table = neighbourhood(node_blocks).reshape(windows, -1, width)
    at_dst = jnp.einsum(
        "en,mnd->med", dst_onehot, node_blocks, preferred_element_type=jnp.float32
    ).astype(jnp.bfloat16)
    local_part = times_plain(jnp.concatenate([edge_rows, at_dst], axis=2), edge_in[: 2 * width])
    at_src = jnp.einsum(
        "en,mnd->med", src_onehot, source_table, preferred_element_type=jnp.float32
    ).astype(jnp.bfloat16)
    act_edge = local_part + times_plain(at_src, edge_in[2 * width :])
    hidden_edge = jax.nn.silu(act_edge).astype(jnp.bfloat16)
    edge_pre = times_plain(hidden_edge, edge_outer)
    message = normalize(edge_pre)[0]
    edge_new = (edge_rows.astype(jnp.float32) + message).astype(jnp.bfloat16)
    summed = onehot_sum("en,med->mnd", dst_onehot, message).astype(jnp.bfloat16)
    node_joined = jnp.concatenate([node_blocks, summed], axis=2)
    act_node = times_plain(node_joined, node_in)
    hidden_node = jax.nn.silu(act_node).astype(jnp.bfloat16)
    node_pre = times_plain(hidden_node, node_outer)
    node_new = (node_blocks.astype(jnp.float32) + normalize(node_pre)[0]).astype(jnp.bfloat16)
    return (node_new, edge_new, (act_edge, edge_pre, act_node, node_pre))


def backward(weights, tables, kept_values, grad_node, grad_edge):
    edge_in, edge_outer, node_in, node_outer = weights
    dst_onehot, src_onehot = tables
    act_edge, edge_pre, act_node, node_pre = kept_values
    windows, block_nodes, width = grad_node.shape
    pre_node_grad = norm_back(node_pre, grad_node).astype(jnp.bfloat16)
    act_node_grad = (times_turned(pre_node_grad, node_outer) * silu_slope(act_node)).astype(
        jnp.bfloat16
    )
    joined_node_grad = times_turned(act_node_grad, node_in)
    message_grad = grad_edge + onehot_sum("en,mnd->med", dst_onehot, joined_node_grad[:, :, width:])
    pre_edge_grad = norm_back(edge_pre, message_grad).astype(jnp.bfloat16)
    act_edge_grad = (times_turned(pre_edge_grad, edge_outer) * silu_slope(act_edge)).astype(
        jnp.bfloat16
    )
    joined_edge_grad = times_turned(act_edge_grad, edge_in)
    edge_back = grad_edge + joined_edge_grad[:, :, :width]
    dst_sums = onehot_sum("en,med->mnd", dst_onehot, joined_edge_grad[:, :, width : 2 * width])
    table_back = onehot_sum("en,med->mnd", src_onehot, joined_edge_grad[:, :, 2 * width :])
    table_back = table_back.reshape(windows, 9, block_nodes, width)
    node_back = (
        grad_node + joined_node_grad[:, :, :width] + dst_sums + return_to_owners(table_back)
    )
    return (node_back, edge_back)


def body(
    node_latents,
    edge_latents,
    tile_offsets,
    edge_dst,
    edge_src,
    edge_in_w,
    edge_out_w,
    node_in_w,
    node_out_w,
    node_cot,
    edge_cot,
):
    windows = node_latents.shape[0]
    block_nodes = node_latents.shape[3]
    width = node_latents.shape[4]
    tile_codes = tile_offsets[0, 0]
    tiles, edges_tile = edge_dst.shape[2:]
    node_iota = lax.broadcasted_iota(jnp.int32, (tiles * edges_tile, block_nodes), 1)
    dst_onehot = (edge_dst.reshape(-1, 1) == node_iota).astype(jnp.bfloat16)
    source_key = (tile_codes[:, None] * block_nodes + edge_src[0, 0]).reshape(-1, 1)
    table_iota = lax.broadcasted_iota(jnp.int32, (tiles * edges_tile, 9 * block_nodes), 1)
    src_onehot = (source_key == table_iota).astype(jnp.bfloat16)
    tables = (dst_onehot, src_onehot)
    is_first = lax.axis_index("phase") == 0
    own = jnp.concatenate([edge_in_w[0], edge_out_w[0], node_in_w[0], node_out_w[0]], axis=0)
    other = lax.ppermute(own, "phase", [(0, 1), (1, 0)])
    sections = (jnp.where(is_first, own, other), jnp.where(is_first, other, own))
    cuts = [0, 3 * width, 4 * width, 6 * width, 7 * width]
    weights = [
        tuple(packed[cuts[i] : cuts[i + 1]] for i in range(4)) for packed in sections
    ]
    def mine(array):
        return lax.dynamic_slice_in_dim(array, lax.axis_index("phase"), 1, axis=0)

    node_zero = mine(node_latents).reshape(1, block_nodes, width)
    edge_zero = mine(edge_latents).reshape(1, -1, width)
    node_one, edge_one, kept_one = forward(weights[0], tables, node_zero, edge_zero)
    node_two, edge_two, kept_two = forward(weights[1], tables, node_one, edge_one)
    latent_send = jnp.where(
        is_first,
        jnp.concatenate([node_two[0], edge_two[0]], axis=0),
        jnp.concatenate([node_one[0], edge_one[0]], axis=0),
    )
    latent_recv = lax.ppermute(latent_send, "phase", [(0, 1), (1, 0)])
    grad_node_one, grad_edge_one = backward(
        weights[1],
        tables,
        kept_two,
        mine(node_cot).reshape(1, block_nodes, width).astype(jnp.float32),
        mine(edge_cot).reshape(1, -1, width).astype(jnp.float32),
    )
    grad_node_zero, grad_edge_zero = backward(
        weights[0], tables, kept_one, grad_node_one, grad_edge_one
    )
    grad_send = jnp.where(
        is_first,
        jnp.concatenate([grad_node_one[0], grad_edge_one[0]], axis=0),
        jnp.concatenate([grad_node_zero[0], grad_edge_zero[0]], axis=0),
    )
    grad_recv = lax.ppermute(grad_send, "phase", [(0, 1), (1, 0)])

    def placed(own_first, own_second, received, shape):
        first = jnp.where(is_first, own_first, received)
        second = jnp.where(is_first, received, own_second)
        return jnp.stack([first, second]).reshape(shape)

    node_shape = (1,) + node_latents.shape
    edge_shape = (1,) + edge_latents.shape
    node_result = placed(node_one[0], node_two[0], latent_recv[:block_nodes], node_shape)
    edge_result = placed(edge_one[0], edge_two[0], latent_recv[block_nodes:], edge_shape)
    node_gradient = placed(
        grad_node_zero[0], grad_node_one[0], grad_recv[:block_nodes], node_shape
    )
    edge_gradient = placed(
        grad_edge_zero[0], grad_edge_one[0], grad_recv[block_nodes:], edge_shape
    )
    return (node_result, edge_result, node_gradient, edge_gradient)


def solution(mesh):
    return jax.shard_map(
        body,
        mesh=mesh,
        in_specs=(
            P(None, "px", "py", None, None),
            P(None, "px", "py", None, None, None),
            P("px", "py", None),
            P("px", "py", None, None),
            P("px", "py", None, None),
            P("phase", None, None),
            P("phase", None, None),
            P("phase", None, None),
            P("phase", None, None),
            P(None, "px", "py", None, None),
            P(None, "px", "py", None, None, None),
        ),
        out_specs=(
            P("phase", None, "px", "py", None, None),
            P("phase", None, "px", "py", None, None, None),
            P("phase", None, "px", "py", None, None),
            P("phase", None, "px", "py", None, None, None),
        ),
        check_vma=False,
    )
```

```python
import jax
import jax.numpy as jnp
from jax import lax
from jax.sharding import PartitionSpec as P


def shifted(array, axis, by):
    count = lax.axis_size(axis)
    pairs = [(i, i + by) for i in range(count) if 0 <= i + by < count]
    return lax.ppermute(array, axis, pairs)


def normalize(values):
    centred = values - jnp.mean(values, axis=-1, keepdims=True)
    inverse = lax.rsqrt(jnp.mean(centred * centred, axis=-1, keepdims=True) + 1e-05)
    return (centred * inverse, inverse)


def norm_back(values, upstream):
    normed, inverse = normalize(values)
    return inverse * (
        upstream
        - jnp.mean(upstream, axis=-1, keepdims=True)
        - normed * jnp.mean(upstream * normed, axis=-1, keepdims=True)
    )


def silu_slope(values):
    squash = jax.nn.sigmoid(values)
    return squash * (1.0 + values * (1.0 - squash))


def times_plain(left, right):
    return jnp.einsum("mrk,kd->mrd", left, right, preferred_element_type=jnp.float32)


def times_turned(left, right):
    return jnp.einsum("mrd,kd->mrk", left, right, preferred_element_type=jnp.float32)


def onehot_sum(form, left, right):
    return jnp.einsum(
        form, left, right, precision=lax.Precision.HIGH, preferred_element_type=jnp.float32
    )


def neighbourhood(node_blocks):
    row = jnp.stack(
        [shifted(node_blocks, "py", 1), node_blocks, shifted(node_blocks, "py", -1)], axis=1
    )
    grid = jnp.stack([shifted(row, "px", 1), row, shifted(row, "px", -1)], axis=1)
    return grid.reshape((grid.shape[0], 9) + grid.shape[3:])


def return_to_owners(table_back):
    grid = table_back.reshape((table_back.shape[0], 3, 3) + table_back.shape[2:])
    low = grid[:, 0].astype(jnp.bfloat16)
    high = grid[:, 2].astype(jnp.bfloat16)
    row = (
        grid[:, 1]
        + shifted(low, "px", -1).astype(jnp.float32)
        + shifted(high, "px", 1).astype(jnp.float32)
    )
    low = row[:, 0].astype(jnp.bfloat16)
    high = row[:, 2].astype(jnp.bfloat16)
    return (
        row[:, 1]
        + shifted(low, "py", -1).astype(jnp.float32)
        + shifted(high, "py", 1).astype(jnp.float32)
    )


def forward(weights, tables, node_blocks, edge_rows):
    edge_in, edge_outer, node_in, node_outer = weights
    dst_onehot, src_onehot = tables
    windows, block_nodes, width = node_blocks.shape
    source_table = neighbourhood(node_blocks).reshape(windows, -1, width)
    at_dst = jnp.einsum(
        "en,mnd->med", dst_onehot, node_blocks, preferred_element_type=jnp.float32
    ).astype(jnp.bfloat16)
    at_src = jnp.einsum(
        "en,mnd->med", src_onehot, source_table, preferred_element_type=jnp.float32
    ).astype(jnp.bfloat16)
    joined = jnp.concatenate([edge_rows, at_dst, at_src], axis=2)
    act_edge = times_plain(joined, edge_in)
    hidden_edge = jax.nn.silu(act_edge).astype(jnp.bfloat16)
    edge_pre = times_plain(hidden_edge, edge_outer)
    message = normalize(edge_pre)[0]
    edge_new = (edge_rows.astype(jnp.float32) + message).astype(jnp.bfloat16)
    summed = onehot_sum("en,med->mnd", dst_onehot, message).astype(jnp.bfloat16)
    node_joined = jnp.concatenate([node_blocks, summed], axis=2)
    act_node = times_plain(node_joined, node_in)
    hidden_node = jax.nn.silu(act_node).astype(jnp.bfloat16)
    node_pre = times_plain(hidden_node, node_outer)
    node_new = (node_blocks.astype(jnp.float32) + normalize(node_pre)[0]).astype(jnp.bfloat16)
    return (node_new, edge_new, (act_edge, edge_pre, act_node, node_pre))


def backward(weights, tables, kept_values, grad_node, grad_edge):
    edge_in, edge_outer, node_in, node_outer = weights
    dst_onehot, src_onehot = tables
    act_edge, edge_pre, act_node, node_pre = kept_values
    windows, block_nodes, width = grad_node.shape
    pre_node_grad = norm_back(node_pre, grad_node).astype(jnp.bfloat16)
    act_node_grad = (times_turned(pre_node_grad, node_outer) * silu_slope(act_node)).astype(
        jnp.bfloat16
    )
    joined_node_grad = times_turned(act_node_grad, node_in)
    message_grad = grad_edge + onehot_sum("en,mnd->med", dst_onehot, joined_node_grad[:, :, width:])
    pre_edge_grad = norm_back(edge_pre, message_grad).astype(jnp.bfloat16)
    act_edge_grad = (times_turned(pre_edge_grad, edge_outer) * silu_slope(act_edge)).astype(
        jnp.bfloat16
    )
    joined_edge_grad = times_turned(act_edge_grad, edge_in)
    edge_back = grad_edge + joined_edge_grad[:, :, :width]
    dst_sums = onehot_sum("en,med->mnd", dst_onehot, joined_edge_grad[:, :, width : 2 * width])
    table_back = onehot_sum("en,med->mnd", src_onehot, joined_edge_grad[:, :, 2 * width :])
    table_back = table_back.reshape(windows, 9, block_nodes, width)
    node_back = (
        grad_node + joined_node_grad[:, :, :width] + dst_sums + return_to_owners(table_back)
    )
    return (node_back, edge_back)


def body(
    node_latents,
    edge_latents,
    tile_offsets,
    edge_dst,
    edge_src,
    edge_in_w,
    edge_out_w,
    node_in_w,
    node_out_w,
    node_cot,
    edge_cot,
):
    windows = node_latents.shape[0]
    block_nodes = node_latents.shape[3]
    width = node_latents.shape[4]
    tile_codes = tile_offsets[0, 0]
    tiles, edges_tile = edge_dst.shape[2:]
    node_iota = lax.broadcasted_iota(jnp.int32, (tiles * edges_tile, block_nodes), 1)
    dst_onehot = (edge_dst.reshape(-1, 1) == node_iota).astype(jnp.bfloat16)
    source_key = (tile_codes[:, None] * block_nodes + edge_src[0, 0]).reshape(-1, 1)
    table_iota = lax.broadcasted_iota(jnp.int32, (tiles * edges_tile, 9 * block_nodes), 1)
    src_onehot = (source_key == table_iota).astype(jnp.bfloat16)
    tables = (dst_onehot, src_onehot)
    is_first = lax.axis_index("phase") == 0
    own = jnp.concatenate([edge_in_w[0], edge_out_w[0], node_in_w[0], node_out_w[0]], axis=0)
    other = lax.ppermute(own, "phase", [(0, 1), (1, 0)])
    sections = (jnp.where(is_first, own, other), jnp.where(is_first, other, own))
    cuts = [0, 3 * width, 4 * width, 6 * width, 7 * width]
    weights = [
        tuple(packed[cuts[i] : cuts[i + 1]] for i in range(4)) for packed in sections
    ]
    def mine(array):
        return jnp.where(is_first, array[0], array[1])[None]

    node_zero = mine(node_latents).reshape(1, block_nodes, width)
    edge_zero = mine(edge_latents).reshape(1, -1, width)
    node_one, edge_one, kept_one = forward(weights[0], tables, node_zero, edge_zero)
    node_two, edge_two, kept_two = forward(weights[1], tables, node_one, edge_one)
    latent_send = jnp.where(
        is_first,
        jnp.concatenate([node_two[0], edge_two[0]], axis=0),
        jnp.concatenate([node_one[0], edge_one[0]], axis=0),
    )
    latent_recv = lax.ppermute(latent_send, "phase", [(0, 1), (1, 0)])
    grad_node_one, grad_edge_one = backward(
        weights[1],
        tables,
        kept_two,
        mine(node_cot).reshape(1, block_nodes, width).astype(jnp.float32),
        mine(edge_cot).reshape(1, -1, width).astype(jnp.float32),
    )
    grad_node_zero, grad_edge_zero = backward(
        weights[0], tables, kept_one, grad_node_one, grad_edge_one
    )
    grad_send = jnp.where(
        is_first,
        jnp.concatenate([grad_node_one[0], grad_edge_one[0]], axis=0),
        jnp.concatenate([grad_node_zero[0], grad_edge_zero[0]], axis=0),
    )
    grad_recv = lax.ppermute(grad_send, "phase", [(0, 1), (1, 0)])

    other_slot = 1 - lax.axis_index("phase")

    def placed(own_first, own_second, received, shape):
        kept = jnp.where(is_first, own_first, own_second)
        pair = jnp.stack([kept, kept])
        pair = lax.dynamic_update_index_in_dim(pair, received, other_slot, axis=0)
        return pair.reshape(shape)

    node_shape = (1,) + node_latents.shape
    edge_shape = (1,) + edge_latents.shape
    node_result = placed(node_one[0], node_two[0], latent_recv[:block_nodes], node_shape)
    edge_result = placed(edge_one[0], edge_two[0], latent_recv[block_nodes:], edge_shape)
    node_gradient = placed(
        grad_node_zero[0], grad_node_one[0], grad_recv[:block_nodes], node_shape
    )
    edge_gradient = placed(
        grad_edge_zero[0], grad_edge_one[0], grad_recv[block_nodes:], edge_shape
    )
    return (node_result, edge_result, node_gradient, edge_gradient)


def solution(mesh):
    return jax.shard_map(
        body,
        mesh=mesh,
        in_specs=(
            P(None, "px", "py", None, None),
            P(None, "px", "py", None, None, None),
            P("px", "py", None),
            P("px", "py", None, None),
            P("px", "py", None, None),
            P("phase", None, None),
            P("phase", None, None),
            P("phase", None, None),
            P("phase", None, None),
            P(None, "px", "py", None, None),
            P(None, "px", "py", None, None, None),
        ),
        out_specs=(
            P("phase", None, "px", "py", None, None),
            P("phase", None, "px", "py", None, None, None),
            P("phase", None, "px", "py", None, None),
            P("phase", None, "px", "py", None, None, None),
        ),
        check_vma=False,
    )
```

```python
import jax
import jax.numpy as jnp
from jax import lax
from jax.sharding import PartitionSpec as P


def shifted(array, axis, by):
    count = lax.axis_size(axis)
    pairs = [(i, i + by) for i in range(count) if 0 <= i + by < count]
    return lax.ppermute(array, axis, pairs)


def normalize(values):
    centred = values - jnp.mean(values, axis=-1, keepdims=True)
    inverse = lax.rsqrt(jnp.mean(centred * centred, axis=-1, keepdims=True) + 1e-05)
    return (centred * inverse, inverse)


def norm_back(values, upstream):
    normed, inverse = normalize(values)
    return inverse * (
        upstream
        - jnp.mean(upstream, axis=-1, keepdims=True)
        - normed * jnp.mean(upstream * normed, axis=-1, keepdims=True)
    )


def silu_slope(values):
    squash = jax.nn.sigmoid(values)
    return squash * (1.0 + values * (1.0 - squash))


def times_plain(left, right):
    return jnp.einsum("mrk,kd->mrd", left, right, preferred_element_type=jnp.float32)


def times_turned(left, right):
    return jnp.einsum("mrd,kd->mrk", left, right, preferred_element_type=jnp.float32)


def onehot_sum(form, left, right):
    return jnp.einsum(
        form, left, right, precision=lax.Precision.HIGH, preferred_element_type=jnp.float32
    )


def neighbourhood(node_blocks):
    row = jnp.stack(
        [shifted(node_blocks, "py", 1), node_blocks, shifted(node_blocks, "py", -1)], axis=1
    )
    grid = jnp.stack([shifted(row, "px", 1), row, shifted(row, "px", -1)], axis=1)
    return grid.reshape((grid.shape[0], 9) + grid.shape[3:])


def return_to_owners(table_back):
    grid = table_back.reshape((table_back.shape[0], 3, 3) + table_back.shape[2:])
    low = grid[:, 0].astype(jnp.bfloat16)
    high = grid[:, 2].astype(jnp.bfloat16)
    row = (
        grid[:, 1]
        + shifted(low, "px", -1).astype(jnp.float32)
        + shifted(high, "px", 1).astype(jnp.float32)
    )
    low = row[:, 0].astype(jnp.bfloat16)
    high = row[:, 2].astype(jnp.bfloat16)
    return (
        row[:, 1]
        + shifted(low, "py", -1).astype(jnp.float32)
        + shifted(high, "py", 1).astype(jnp.float32)
    )


def forward(weights, tables, node_blocks, edge_rows):
    edge_in, edge_outer, node_in, node_outer = weights
    dst_onehot, src_onehot = tables
    windows, block_nodes, width = node_blocks.shape
    source_table = neighbourhood(node_blocks).reshape(windows, -1, width)
    at_dst = jnp.einsum(
        "en,mnd->med", dst_onehot, node_blocks, preferred_element_type=jnp.float32
    ).astype(jnp.bfloat16)
    at_src = jnp.einsum(
        "en,mnd->med", src_onehot, source_table, preferred_element_type=jnp.float32
    ).astype(jnp.bfloat16)
    joined = jnp.concatenate([edge_rows, at_dst, at_src], axis=2)
    act_edge = times_plain(joined, edge_in)
    hidden_edge = jax.nn.silu(act_edge).astype(jnp.bfloat16)
    edge_pre = times_plain(hidden_edge, edge_outer)
    message = normalize(edge_pre)[0]
    edge_new = (edge_rows.astype(jnp.float32) + message).astype(jnp.bfloat16)
    summed = onehot_sum("en,med->mnd", dst_onehot, message).astype(jnp.bfloat16)
    node_joined = jnp.concatenate([node_blocks, summed], axis=2)
    act_node = times_plain(node_joined, node_in)
    hidden_node = jax.nn.silu(act_node).astype(jnp.bfloat16)
    node_pre = times_plain(hidden_node, node_outer)
    node_new = (node_blocks.astype(jnp.float32) + normalize(node_pre)[0]).astype(jnp.bfloat16)
    return (node_new, edge_new, (act_edge, edge_pre, act_node, node_pre))


def backward(weights, tables, kept_values, grad_node, grad_edge):
    edge_in, edge_outer, node_in, node_outer = weights
    dst_onehot, src_onehot = tables
    act_edge, edge_pre, act_node, node_pre = kept_values
    windows, block_nodes, width = grad_node.shape
    pre_node_grad = norm_back(node_pre, grad_node).astype(jnp.bfloat16)
    act_node_grad = (times_turned(pre_node_grad, node_outer) * silu_slope(act_node)).astype(
        jnp.bfloat16
    )
    joined_node_grad = times_turned(act_node_grad, node_in)
    message_grad = grad_edge + onehot_sum("en,mnd->med", dst_onehot, joined_node_grad[:, :, width:])
    pre_edge_grad = norm_back(edge_pre, message_grad).astype(jnp.bfloat16)
    act_edge_grad = (times_turned(pre_edge_grad, edge_outer) * silu_slope(act_edge)).astype(
        jnp.bfloat16
    )
    joined_edge_grad = times_turned(act_edge_grad, edge_in)
    edge_back = grad_edge + joined_edge_grad[:, :, :width]
    dst_sums = onehot_sum("en,med->mnd", dst_onehot, joined_edge_grad[:, :, width : 2 * width])
    table_back = onehot_sum("en,med->mnd", src_onehot, joined_edge_grad[:, :, 2 * width :])
    table_back = table_back.reshape(windows, 9, block_nodes, width)
    node_back = (
        grad_node + joined_node_grad[:, :, :width] + dst_sums + return_to_owners(table_back)
    )
    return (node_back, edge_back)


def body(
    node_latents,
    edge_latents,
    tile_offsets,
    edge_dst,
    edge_src,
    edge_in_w,
    edge_out_w,
    node_in_w,
    node_out_w,
    node_cot,
    edge_cot,
):
    windows = node_latents.shape[0]
    block_nodes = node_latents.shape[3]
    width = node_latents.shape[4]
    tile_codes = tile_offsets[0, 0]
    tiles, edges_tile = edge_dst.shape[2:]
    node_iota = lax.broadcasted_iota(jnp.int32, (tiles * edges_tile, block_nodes), 1)
    dst_onehot = (edge_dst.reshape(-1, 1) == node_iota).astype(jnp.bfloat16)
    source_key = (tile_codes[:, None] * block_nodes + edge_src[0, 0]).reshape(-1, 1)
    table_iota = lax.broadcasted_iota(jnp.int32, (tiles * edges_tile, 9 * block_nodes), 1)
    src_onehot = (source_key == table_iota).astype(jnp.bfloat16)
    tables = (dst_onehot, src_onehot)
    is_first = lax.axis_index("phase") == 0
    own = jnp.concatenate([edge_in_w[0], edge_out_w[0], node_in_w[0], node_out_w[0]], axis=0)
    other = lax.ppermute(own, "phase", [(0, 1), (1, 0)])
    sections = (jnp.where(is_first, own, other), jnp.where(is_first, other, own))
    cuts = [0, 3 * width, 4 * width, 6 * width, 7 * width]
    weights = [
        tuple(packed[cuts[i] : cuts[i + 1]] for i in range(4)) for packed in sections
    ]
    def mine(array):
        return jnp.where(is_first, array[0], array[1])[None]

    node_zero = mine(node_latents).reshape(1, block_nodes, width)
    edge_zero = mine(edge_latents).reshape(1, -1, width)
    node_one, edge_one, kept_one = forward(weights[0], tables, node_zero, edge_zero)
    node_two, edge_two, kept_two = forward(weights[1], tables, node_one, edge_one)
    grad_node_one, grad_edge_one = backward(
        weights[1],
        tables,
        kept_two,
        mine(node_cot).reshape(1, block_nodes, width).astype(jnp.float32),
        mine(edge_cot).reshape(1, -1, width).astype(jnp.float32),
    )
    grad_node_zero, grad_edge_zero = backward(
        weights[0], tables, kept_one, grad_node_one, grad_edge_one
    )
    swap_send = jnp.where(
        is_first,
        jnp.concatenate(
            [node_two[0], edge_two[0], grad_node_one[0], grad_edge_one[0]], axis=0
        ),
        jnp.concatenate(
            [node_one[0], edge_one[0], grad_node_zero[0], grad_edge_zero[0]], axis=0
        ),
    )
    swap_recv = lax.ppermute(swap_send, "phase", [(0, 1), (1, 0)])
    rows = block_nodes + edge_zero.shape[1]
    latent_recv = swap_recv[:rows].astype(jnp.bfloat16)
    grad_recv = swap_recv[rows:]

    def placed(own_first, own_second, received, shape):
        kept = jnp.where(is_first, own_first, own_second)
        pair = jnp.where(
            is_first, jnp.stack([kept, received]), jnp.stack([received, kept])
        )
        return pair.reshape(shape)

    node_shape = (1,) + node_latents.shape
    edge_shape = (1,) + edge_latents.shape
    node_result = placed(node_one[0], node_two[0], latent_recv[:block_nodes], node_shape)
    edge_result = placed(edge_one[0], edge_two[0], latent_recv[block_nodes:], edge_shape)
    node_gradient = placed(
        grad_node_zero[0], grad_node_one[0], grad_recv[:block_nodes], node_shape
    )
    edge_gradient = placed(
        grad_edge_zero[0], grad_edge_one[0], grad_recv[block_nodes:], edge_shape
    )
    return (node_result, edge_result, node_gradient, edge_gradient)


def solution(mesh):
    return jax.shard_map(
        body,
        mesh=mesh,
        in_specs=(
            P(None, "px", "py", None, None),
            P(None, "px", "py", None, None, None),
            P("px", "py", None),
            P("px", "py", None, None),
            P("px", "py", None, None),
            P("phase", None, None),
            P("phase", None, None),
            P("phase", None, None),
            P("phase", None, None),
            P(None, "px", "py", None, None),
            P(None, "px", "py", None, None, None),
        ),
        out_specs=(
            P("phase", None, "px", "py", None, None),
            P("phase", None, "px", "py", None, None, None),
            P("phase", None, "px", "py", None, None),
            P("phase", None, "px", "py", None, None, None),
        ),
        check_vma=False,
    )
```

```python
import jax
import jax.numpy as jnp
from jax import lax
from jax.sharding import PartitionSpec as P


def shifted(array, axis, by):
    count = lax.axis_size(axis)
    pairs = [(i, i + by) for i in range(count) if 0 <= i + by < count]
    return lax.ppermute(array, axis, pairs)


def normalize(values):
    centred = values - jnp.mean(values, axis=-1, keepdims=True)
    inverse = lax.rsqrt(jnp.mean(centred * centred, axis=-1, keepdims=True) + 1e-05)
    return (centred * inverse, inverse)


def norm_back(values, upstream):
    normed, inverse = normalize(values)
    return inverse * (
        upstream
        - jnp.mean(upstream, axis=-1, keepdims=True)
        - normed * jnp.mean(upstream * normed, axis=-1, keepdims=True)
    )


def silu_slope(values):
    squash = jax.nn.sigmoid(values)
    return squash * (1.0 + values * (1.0 - squash))


def times_plain(left, right):
    return jnp.einsum("mrk,kd->mrd", left, right, preferred_element_type=jnp.float32)


def times_turned(left, right):
    return jnp.einsum("mrd,kd->mrk", left, right, preferred_element_type=jnp.float32)


def onehot_sum(form, left, right):
    return jnp.einsum(
        form, left, right, precision=lax.Precision.HIGH, preferred_element_type=jnp.float32
    )


def neighbourhood(node_blocks):
    row = jnp.stack(
        [shifted(node_blocks, "py", 1), node_blocks, shifted(node_blocks, "py", -1)], axis=1
    )
    grid = jnp.stack([shifted(row, "px", 1), row, shifted(row, "px", -1)], axis=1)
    return grid.reshape((grid.shape[0], 9) + grid.shape[3:])


def return_to_owners(table_back):
    grid = table_back.reshape((table_back.shape[0], 3, 3) + table_back.shape[2:])
    low = grid[:, 0].astype(jnp.bfloat16)
    high = grid[:, 2].astype(jnp.bfloat16)
    row = (
        grid[:, 1]
        + shifted(low, "px", -1).astype(jnp.float32)
        + shifted(high, "px", 1).astype(jnp.float32)
    )
    low = row[:, 0].astype(jnp.bfloat16)
    high = row[:, 2].astype(jnp.bfloat16)
    return (
        row[:, 1]
        + shifted(low, "py", -1).astype(jnp.float32)
        + shifted(high, "py", 1).astype(jnp.float32)
    )


def forward(weights, tables, node_blocks, edge_rows):
    edge_in, edge_outer, node_in, node_outer = weights
    dst_onehot, src_onehot = tables
    windows, block_nodes, width = node_blocks.shape
    source_table = neighbourhood(node_blocks).reshape(windows, -1, width)
    at_dst = jnp.einsum(
        "en,mnd->med", dst_onehot, node_blocks, preferred_element_type=jnp.float32
    ).astype(jnp.bfloat16)
    at_src = jnp.einsum(
        "en,mnd->med", src_onehot, source_table, preferred_element_type=jnp.float32
    ).astype(jnp.bfloat16)
    joined = jnp.concatenate([edge_rows, at_dst, at_src], axis=2)
    act_edge = times_plain(joined, edge_in)
    hidden_edge = jax.nn.silu(act_edge).astype(jnp.bfloat16)
    edge_pre = times_plain(hidden_edge, edge_outer)
    message = normalize(edge_pre)[0]
    edge_new = (edge_rows.astype(jnp.float32) + message).astype(jnp.bfloat16)
    summed = onehot_sum("en,med->mnd", dst_onehot, message).astype(jnp.bfloat16)
    node_joined = jnp.concatenate([node_blocks, summed], axis=2)
    act_node = times_plain(node_joined, node_in)
    hidden_node = jax.nn.silu(act_node).astype(jnp.bfloat16)
    node_pre = times_plain(hidden_node, node_outer)
    node_new = (node_blocks.astype(jnp.float32) + normalize(node_pre)[0]).astype(jnp.bfloat16)
    return (node_new, edge_new, (act_edge, edge_pre, act_node, node_pre))


def backward(weights, tables, kept_values, grad_node, grad_edge):
    edge_in, edge_outer, node_in, node_outer = weights
    dst_onehot, src_onehot = tables
    act_edge, edge_pre, act_node, node_pre = kept_values
    windows, block_nodes, width = grad_node.shape
    pre_node_grad = norm_back(node_pre, grad_node).astype(jnp.bfloat16)
    act_node_grad = (times_turned(pre_node_grad, node_outer) * silu_slope(act_node)).astype(
        jnp.bfloat16
    )
    joined_node_grad = times_turned(act_node_grad, node_in)
    message_grad = grad_edge + onehot_sum("en,mnd->med", dst_onehot, joined_node_grad[:, :, width:])
    pre_edge_grad = norm_back(edge_pre, message_grad).astype(jnp.bfloat16)
    act_edge_grad = (times_turned(pre_edge_grad, edge_outer) * silu_slope(act_edge)).astype(
        jnp.bfloat16
    )
    joined_edge_grad = times_turned(act_edge_grad, edge_in)
    edge_back = grad_edge + joined_edge_grad[:, :, :width]
    dst_sums = onehot_sum("en,med->mnd", dst_onehot, joined_edge_grad[:, :, width : 2 * width])
    table_back = onehot_sum("en,med->mnd", src_onehot, joined_edge_grad[:, :, 2 * width :])
    table_back = table_back.reshape(windows, 9, block_nodes, width)
    node_back = (
        grad_node + joined_node_grad[:, :, :width] + dst_sums + return_to_owners(table_back)
    )
    return (node_back, edge_back)


def body(
    node_latents,
    edge_latents,
    tile_offsets,
    edge_dst,
    edge_src,
    edge_in_w,
    edge_out_w,
    node_in_w,
    node_out_w,
    node_cot,
    edge_cot,
):
    windows = node_latents.shape[0]
    block_nodes = node_latents.shape[3]
    width = node_latents.shape[4]
    tile_codes = tile_offsets[0, 0]
    tiles, edges_tile = edge_dst.shape[2:]
    node_iota = lax.broadcasted_iota(jnp.int32, (tiles * edges_tile, block_nodes), 1)
    dst_onehot = (edge_dst.reshape(-1, 1) == node_iota).astype(jnp.bfloat16)
    source_key = (tile_codes[:, None] * block_nodes + edge_src[0, 0]).reshape(-1, 1)
    table_iota = lax.broadcasted_iota(jnp.int32, (tiles * edges_tile, 9 * block_nodes), 1)
    src_onehot = (source_key == table_iota).astype(jnp.bfloat16)
    tables = (dst_onehot, src_onehot)
    is_first = lax.axis_index("phase") == 0
    own = jnp.concatenate([edge_in_w[0], edge_out_w[0], node_in_w[0], node_out_w[0]], axis=0)
    other = lax.ppermute(own, "phase", [(0, 1), (1, 0)])
    sections = (jnp.where(is_first, own, other), jnp.where(is_first, other, own))
    cuts = [0, 3 * width, 4 * width, 6 * width, 7 * width]
    weights = [
        tuple(packed[cuts[i] : cuts[i + 1]] for i in range(4)) for packed in sections
    ]
    def mine(array):
        return jnp.where(is_first, array[0], array[1])[None]

    node_zero = mine(node_latents).reshape(1, block_nodes, width)
    edge_zero = mine(edge_latents).reshape(1, -1, width)
    node_one, edge_one, kept_one = forward(weights[0], tables, node_zero, edge_zero)
    node_two, edge_two, kept_two = forward(weights[1], tables, node_one, edge_one)
    grad_node_one, grad_edge_one = backward(
        weights[1],
        tables,
        kept_two,
        mine(node_cot).reshape(1, block_nodes, width).astype(jnp.float32),
        mine(edge_cot).reshape(1, -1, width).astype(jnp.float32),
    )
    grad_node_zero, grad_edge_zero = backward(
        weights[0], tables, kept_one, grad_node_one, grad_edge_one
    )
    swap_send = jnp.where(
        is_first,
        jnp.concatenate(
            [node_two[0], edge_two[0], grad_node_one[0], grad_edge_one[0]], axis=0
        ),
        jnp.concatenate(
            [node_one[0], edge_one[0], grad_node_zero[0], grad_edge_zero[0]], axis=0
        ),
    )
    swap_recv = lax.ppermute(swap_send, "phase", [(0, 1), (1, 0)])
    rows = block_nodes + edge_zero.shape[1]
    latent_recv = swap_recv[:rows].astype(jnp.bfloat16)
    grad_recv = swap_recv[rows:]

    other_slot = 1 - lax.axis_index("phase")

    def placed(own_first, own_second, received, shape):
        kept = jnp.where(is_first, own_first, own_second)
        pair = jnp.stack([kept, kept])
        pair = lax.dynamic_update_index_in_dim(pair, received, other_slot, axis=0)
        return pair.reshape(shape)

    node_shape = (1,) + node_latents.shape
    edge_shape = (1,) + edge_latents.shape
    node_result = placed(node_one[0], node_two[0], latent_recv[:block_nodes], node_shape)
    edge_result = placed(edge_one[0], edge_two[0], latent_recv[block_nodes:], edge_shape)
    node_gradient = placed(
        grad_node_zero[0], grad_node_one[0], grad_recv[:block_nodes], node_shape
    )
    edge_gradient = placed(
        grad_edge_zero[0], grad_edge_one[0], grad_recv[block_nodes:], edge_shape
    )
    return (node_result, edge_result, node_gradient, edge_gradient)


def solution(mesh):
    return jax.shard_map(
        body,
        mesh=mesh,
        in_specs=(
            P(None, "px", "py", None, None),
            P(None, "px", "py", None, None, None),
            P("px", "py", None),
            P("px", "py", None, None),
            P("px", "py", None, None),
            P("phase", None, None),
            P("phase", None, None),
            P("phase", None, None),
            P("phase", None, None),
            P(None, "px", "py", None, None),
            P(None, "px", "py", None, None, None),
        ),
        out_specs=(
            P("phase", None, "px", "py", None, None),
            P("phase", None, "px", "py", None, None, None),
            P("phase", None, "px", "py", None, None),
            P("phase", None, "px", "py", None, None, None),
        ),
        check_vma=False,
    )
```

```python
import jax
import jax.numpy as jnp
from jax import lax
from jax.sharding import PartitionSpec as P


def shifted(array, axis, by):
    count = lax.axis_size(axis)
    pairs = [(i, i + by) for i in range(count) if 0 <= i + by < count]
    return lax.ppermute(array, axis, pairs)


def normalize(values):
    centred = values - jnp.mean(values, axis=-1, keepdims=True)
    inverse = lax.rsqrt(jnp.mean(centred * centred, axis=-1, keepdims=True) + 1e-05)
    return (centred * inverse, inverse)


def norm_back(values, upstream):
    normed, inverse = normalize(values)
    return inverse * (
        upstream
        - jnp.mean(upstream, axis=-1, keepdims=True)
        - normed * jnp.mean(upstream * normed, axis=-1, keepdims=True)
    )


def silu_slope(values):
    squash = jax.nn.sigmoid(values)
    return squash * (1.0 + values * (1.0 - squash))


def times_plain(left, right):
    return jnp.einsum("mrk,kd->mrd", left, right, preferred_element_type=jnp.float32)


def times_turned(left, right):
    return jnp.einsum("mrd,kd->mrk", left, right, preferred_element_type=jnp.float32)


def onehot_sum(form, left, right):
    return jnp.einsum(
        form, left, right, precision=lax.Precision.HIGH, preferred_element_type=jnp.float32
    )


def neighbourhood(node_blocks):
    row = jnp.stack(
        [shifted(node_blocks, "py", 1), node_blocks, shifted(node_blocks, "py", -1)], axis=1
    )
    grid = jnp.stack([shifted(row, "px", 1), row, shifted(row, "px", -1)], axis=1)
    return grid.reshape((grid.shape[0], 9) + grid.shape[3:])


def return_to_owners(table_back):
    grid = table_back.reshape((table_back.shape[0], 3, 3) + table_back.shape[2:])
    low = grid[:, 0].astype(jnp.bfloat16)
    high = grid[:, 2].astype(jnp.bfloat16)
    row = (
        grid[:, 1]
        + shifted(low, "px", -1).astype(jnp.float32)
        + shifted(high, "px", 1).astype(jnp.float32)
    )
    low = row[:, 0].astype(jnp.bfloat16)
    high = row[:, 2].astype(jnp.bfloat16)
    return (
        row[:, 1]
        + shifted(low, "py", -1).astype(jnp.float32)
        + shifted(high, "py", 1).astype(jnp.float32)
    )


def forward(weights, tables, node_blocks, edge_rows):
    edge_in, edge_outer, node_in, node_outer = weights
    dst_onehot, src_onehot = tables
    windows, block_nodes, width = node_blocks.shape
    source_table = neighbourhood(node_blocks).reshape(windows, -1, width)
    at_dst = jnp.einsum(
        "en,mnd->med", dst_onehot, node_blocks, preferred_element_type=jnp.float32
    ).astype(jnp.bfloat16)
    at_src = jnp.einsum(
        "en,mnd->med", src_onehot, source_table, preferred_element_type=jnp.float32
    ).astype(jnp.bfloat16)
    joined = jnp.concatenate([edge_rows, at_dst, at_src], axis=2)
    act_edge = times_plain(joined, edge_in)
    hidden_edge = jax.nn.silu(act_edge).astype(jnp.bfloat16)
    edge_pre = times_plain(hidden_edge, edge_outer)
    message = normalize(edge_pre)[0]
    edge_new = (edge_rows.astype(jnp.float32) + message).astype(jnp.bfloat16)
    summed = onehot_sum("en,med->mnd", dst_onehot, message).astype(jnp.bfloat16)
    node_joined = jnp.concatenate([node_blocks, summed], axis=2)
    act_node = times_plain(node_joined, node_in)
    hidden_node = jax.nn.silu(act_node).astype(jnp.bfloat16)
    node_pre = times_plain(hidden_node, node_outer)
    node_new = (node_blocks.astype(jnp.float32) + normalize(node_pre)[0]).astype(jnp.bfloat16)
    return (node_new, edge_new, (act_edge, edge_pre, act_node, node_pre))


def backward(weights, tables, kept_values, grad_node, grad_edge):
    edge_in, edge_outer, node_in, node_outer = weights
    dst_onehot, src_onehot = tables
    act_edge, edge_pre, act_node, node_pre = kept_values
    windows, block_nodes, width = grad_node.shape
    pre_node_grad = norm_back(node_pre, grad_node).astype(jnp.bfloat16)
    act_node_grad = (times_turned(pre_node_grad, node_outer) * silu_slope(act_node)).astype(
        jnp.bfloat16
    )
    joined_node_grad = times_turned(act_node_grad, node_in)
    message_grad = grad_edge + onehot_sum("en,mnd->med", dst_onehot, joined_node_grad[:, :, width:])
    pre_edge_grad = norm_back(edge_pre, message_grad).astype(jnp.bfloat16)
    act_edge_grad = (times_turned(pre_edge_grad, edge_outer) * silu_slope(act_edge)).astype(
        jnp.bfloat16
    )
    joined_edge_grad = times_turned(act_edge_grad, edge_in)
    edge_back = grad_edge + joined_edge_grad[:, :, :width]
    dst_sums = onehot_sum("en,med->mnd", dst_onehot, joined_edge_grad[:, :, width : 2 * width])
    table_back = onehot_sum("en,med->mnd", src_onehot, joined_edge_grad[:, :, 2 * width :])
    table_back = table_back.reshape(windows, 9, block_nodes, width)
    node_back = (
        grad_node + joined_node_grad[:, :, :width] + dst_sums + return_to_owners(table_back)
    )
    return (node_back, edge_back)


def body(
    node_latents,
    edge_latents,
    tile_offsets,
    edge_dst,
    edge_src,
    edge_in_w,
    edge_out_w,
    node_in_w,
    node_out_w,
    node_cot,
    edge_cot,
):
    windows = node_latents.shape[0]
    block_nodes = node_latents.shape[3]
    width = node_latents.shape[4]
    tile_codes = tile_offsets[0, 0]
    tiles, edges_tile = edge_dst.shape[2:]
    node_iota = lax.broadcasted_iota(jnp.int32, (tiles * edges_tile, block_nodes), 1)
    dst_onehot = (edge_dst.reshape(-1, 1) == node_iota).astype(jnp.bfloat16)
    source_key = (tile_codes[:, None] * block_nodes + edge_src[0, 0]).reshape(-1, 1)
    table_iota = lax.broadcasted_iota(jnp.int32, (tiles * edges_tile, 9 * block_nodes), 1)
    src_onehot = (source_key == table_iota).astype(jnp.bfloat16)
    tables = (dst_onehot, src_onehot)
    is_first = lax.axis_index("phase") == 0
    own = jnp.concatenate([edge_in_w[0], edge_out_w[0], node_in_w[0], node_out_w[0]], axis=0)
    other = lax.ppermute(own, "phase", [(0, 1), (1, 0)])
    sections = (jnp.where(is_first, own, other), jnp.where(is_first, other, own))
    cuts = [0, 3 * width, 4 * width, 6 * width, 7 * width]
    weights = [
        tuple(packed[cuts[i] : cuts[i + 1]] for i in range(4)) for packed in sections
    ]
    def mine(array):
        return lax.dynamic_slice_in_dim(array, lax.axis_index("phase"), 1, axis=0)

    node_zero = mine(node_latents).reshape(1, block_nodes, width)
    edge_zero = mine(edge_latents).reshape(1, -1, width)
    node_one, edge_one, kept_one = forward(weights[0], tables, node_zero, edge_zero)
    node_two, edge_two, kept_two = forward(weights[1], tables, node_one, edge_one)
    grad_node_one, grad_edge_one = backward(
        weights[1],
        tables,
        kept_two,
        mine(node_cot).reshape(1, block_nodes, width).astype(jnp.float32),
        mine(edge_cot).reshape(1, -1, width).astype(jnp.float32),
    )
    grad_node_zero, grad_edge_zero = backward(
        weights[0], tables, kept_one, grad_node_one, grad_edge_one
    )
    swap_send = jnp.where(
        is_first,
        jnp.concatenate(
            [node_two[0], edge_two[0], grad_node_one[0], grad_edge_one[0]], axis=0
        ),
        jnp.concatenate(
            [node_one[0], edge_one[0], grad_node_zero[0], grad_edge_zero[0]], axis=0
        ),
    )
    swap_recv = lax.ppermute(swap_send, "phase", [(0, 1), (1, 0)])
    rows = block_nodes + edge_zero.shape[1]
    latent_recv = swap_recv[:rows].astype(jnp.bfloat16)
    grad_recv = swap_recv[rows:]

    other_slot = 1 - lax.axis_index("phase")

    def placed(own_first, own_second, received, shape):
        kept = jnp.where(is_first, own_first, own_second)
        pair = jnp.stack([kept, kept])
        pair = lax.dynamic_update_index_in_dim(pair, received, other_slot, axis=0)
        return pair.reshape(shape)

    node_shape = (1,) + node_latents.shape
    edge_shape = (1,) + edge_latents.shape
    node_result = placed(node_one[0], node_two[0], latent_recv[:block_nodes], node_shape)
    edge_result = placed(edge_one[0], edge_two[0], latent_recv[block_nodes:], edge_shape)
    node_gradient = placed(
        grad_node_zero[0], grad_node_one[0], grad_recv[:block_nodes], node_shape
    )
    edge_gradient = placed(
        grad_edge_zero[0], grad_edge_one[0], grad_recv[block_nodes:], edge_shape
    )
    return (node_result, edge_result, node_gradient, edge_gradient)


def solution(mesh):
    return jax.shard_map(
        body,
        mesh=mesh,
        in_specs=(
            P(None, "px", "py", None, None),
            P(None, "px", "py", None, None, None),
            P("px", "py", None),
            P("px", "py", None, None),
            P("px", "py", None, None),
            P("phase", None, None),
            P("phase", None, None),
            P("phase", None, None),
            P("phase", None, None),
            P(None, "px", "py", None, None),
            P(None, "px", "py", None, None, None),
        ),
        out_specs=(
            P("phase", None, "px", "py", None, None),
            P("phase", None, "px", "py", None, None, None),
            P("phase", None, "px", "py", None, None),
            P("phase", None, "px", "py", None, None, None),
        ),
        check_vma=False,
    )
```
